256 devices in a mesh: section: 16 (over x, z_lo), expert: 16 (over y, z_hi, core).
Axes of the slice: x: 4, y: 4, z: 8 (z_hi: 2, z_lo: 4; z = z_hi * 4 + z_lo), core: 2. Of those that a mesh axis runs over, the one named last changes fastest.
Arguments:
- stream: bfloat16 [16, 256, 4096], P('section', 'expert'), may hold values from -6 to 6
- queries: bfloat16 [16, 256, 4096], P('section', None, 'expert'), may hold values from -6 to 6
- keyvals: bfloat16 [16, 4096, 512], P('section', 'expert'), may hold values from -6 to 6
- w_out: bfloat16 [16, 4096, 4096], P('section', 'expert'), may hold values from -0.5 to 0.5
- norm_gain: float32 [16, 4096], P('section'), may hold values from 0.5 to 1.5
- w_gate: bfloat16 [16, 4096, 6144], P('section', None, 'expert'), may hold values from -0.09375 to 0.09375
- w_up: bfloat16 [16, 4096, 6144], P('section', None, 'expert'), may hold values from -0.09375 to 0.09375
- w_down: bfloat16 [16, 6144, 4096], P('section', 'expert'), may hold values from -0.3125 to 0.3125
- routes: int32 [16, 256, 2], P('section'), may hold values from 0 to 3, all different within a row; in each aligned block of 16 rows (0 to 15, 16 to 31, ..., all dimensions but the last counted through in order) at most 12 rows name the same one
- gate_scores: float32 [16, 256, 2], P('section'), may hold values from 0.05 to 20
Outputs:
- passed: bfloat16 [16, 256, 4096], P('section', 'expert')
The draws below stay inside these ranges and needn't reach their ends.
Inputs may be any that keep to these rules, and one draw needn't show every extreme that they name: `routes`: each row names 2 different experts. In each aligned block of 16 rows (the tokens of one device) no expert is named by more than 12 rows.
All inputs are finite; a program needn't handle non-finite values.
Results may differ from the reference program's by a relative error of at most 0.02.
Values may be sent and summed in bfloat16 or wider, within the bound.
No kernel may reach another device: no remote copies, remote signals or barrier semaphores. Data moves between devices by JAX's collectives and lax.ppermute only.
A program may use at most 64 MiB of HBM per device.

```python
import math
import jax
import jax.numpy as jnp
import numpy as np
from jax import lax

D = 4096
HD = 128
FF = 1536
QHEADS = 32
KVHEADS = 2
HID_DEV = 384
CTX = 4096
MB = 256
SECTIONS = 16
TOK = 16
SPLIT = 4
EXPERTS = 4
TOPK = 2
CAP = 12
N_EXPERT = 16


def draw_queries(key, part):
    shape = (SECTIONS, MB, QHEADS * HD)
    field = jnp.clip(jax.random.normal(jax.random.fold_in(key, 11), shape, jnp.float32), -6.0, 6.0)
    return field.astype(jnp.bfloat16)


def draw_keyvals(key, part):
    shape = (SECTIONS, CTX, KVHEADS * 2 * HD)
    field = jnp.clip(jax.random.normal(jax.random.fold_in(key, 23), shape, jnp.float32), -6.0, 6.0)
    return field.astype(jnp.bfloat16)


def levels(key, extent, split, low, high):
    factor_of, own = 1.0, jax.random.fold_in(key, 6)
    for position, blocks in split:
        draws = jnp.exp(jax.random.uniform(jax.random.fold_in(own, position), (blocks,), jnp.float32, low / len(split), high / len(split)))
        factor_of = factor_of * jnp.repeat(draws, extent[position] // blocks).reshape([-1 if axis == position else 1 for axis in range(len(extent))])
    return factor_of


def assign_block(own_key, own, number, rows, amount, top, limit, lean):
    ranking = jax.random.permutation(own_key, amount)
    packed, ordinary = portions_of(amount, rows * top, limit, lean, True), portions_of(amount, rows * top, limit, lean, False)
    places = jnp.arange(amount)

    def named(lengths, rotation):
        used = int((lengths > 0).sum())
        fixed = max(1, used // 4)
        shifted = fixed + (places - fixed + rotation * (used - fixed)) % max(1, amount - fixed)
        return jnp.zeros((amount,), jnp.int32).at[ranking[jnp.where(places < fixed, places, shifted)]].set(jnp.asarray(lengths, jnp.int32))

    lengths = jnp.where(number % 4 == 0, named(packed, number // 4), named(ordinary, number - number // 4 - 1))
    mixed = jax.random.permutation(jax.random.fold_in(own, 3), amount)
    donor, receiver = mixed[0:amount // 2 * 2:2], mixed[1:amount // 2 * 2:2]
    room = jnp.minimum(lengths[donor] - 1, limit - lengths[receiver]) // 2
    room = jnp.where((donor == ranking[0]) | (receiver == ranking[0]) | (lengths[receiver] == 0), 0, jnp.maximum(room, 0))
    shifted = jax.random.randint(jax.random.fold_in(own, 4), (amount // 2,), 0, 1 << 20) % (room + 1)
    lengths = lengths.at[donor].add(-shifted).at[receiver].add(shifted)
    items = jnp.searchsorted(jnp.cumsum(lengths), jnp.arange(rows * top), side="right").astype(jnp.int32)
    grid = items.reshape(top, rows).T
    grid = grid[jax.random.permutation(jax.random.fold_in(own, 1), rows)]
    rotation = jax.random.randint(jax.random.fold_in(own, 2), (rows, 1), 0, top)
    return jnp.take_along_axis(grid, (jnp.arange(top)[None, :] + rotation) % top, axis=1)


def portions_of(amount, total, reach, slope, full):
    weights = [(1 << 20) // math.isqrt(grade ** slope) + 1 for grade in range(1, amount + 1)]
    largest = reach if full else min(reach, max(-(-total // amount), total * weights[0] // sum(weights)))
    least = 1 if total - largest >= amount - 1 else 0
    given, surplus = [largest] + [least] * (amount - 1), total - largest - least * (amount - 1)
    while surplus > 0:
        free = [i for i in range(1, amount) if given[i] < largest] or [i for i in range(1, amount) if given[i] < reach]
        mass, budget = sum([weights[i] for i in free]), surplus
        for i in free:
            more = min(reach - given[i], max(1, budget * weights[i] // mass), surplus)
            given[i] = given[i] + more
            surplus = surplus - more
    return np.array(given)


def bell_draw(own_key, dims, spread, most, cuts=(), kind=jnp.bfloat16):
    values = jax.random.normal(own_key, dims, jnp.float32) * spread
    if len(cuts) > 0:
        values = levels(own_key, dims, cuts, -0.22, 0.18) * values
    return jnp.clip(values, min=-most, max=most).astype(kind)


def setup_inputs(seed: int = 0) -> dict:
    splits = jax.random.split(jax.random.key(seed), 11)
    stream = bell_draw(splits[0], (SECTIONS, MB, D), 1.0, 6.0, ((0, 16), (1, 16)))
    queries = draw_queries(jax.random.fold_in(splits[10], 71), 0)
    keyvals = draw_keyvals(jax.random.fold_in(splits[10], 71), 0)
    w_out = bell_draw(splits[3], (SECTIONS, QHEADS * HD, D), HD ** -0.5, 0.5, ((0, 16), (1, 16)))
    norm_gain = jnp.clip(1.0 + 0.1 * jax.random.normal(splits[4], (SECTIONS, D), jnp.float32), 0.5, 1.5)
    w_gate = bell_draw(splits[5], (SECTIONS, D, EXPERTS * FF), D ** -0.5, 0.09375, ((0, 16), (2, 16)))
    w_up = bell_draw(splits[6], (SECTIONS, D, EXPERTS * FF), D ** -0.5, 0.09375, ((0, 16), (2, 16)))
    w_down = bell_draw(splits[7], (SECTIONS, EXPERTS * FF, D), HID_DEV ** -0.5, 0.3125, ((0, 16), (1, 16)))
    routes_keys = jax.random.split(jax.random.fold_in(splits[8], 1), SECTIONS * MB // TOK)
    routes_turns = jax.random.permutation(jax.random.fold_in(splits[8], 3), SECTIONS * MB // TOK)
    routes = jax.vmap(lambda own, number: assign_block(jax.random.fold_in(splits[8], 2), own, number, TOK, EXPERTS, TOPK, CAP, 2))(routes_keys, routes_turns).reshape((SECTIONS, MB, TOPK))
    gate_scores = jnp.clip(jnp.exp(math.log(20.0) - 5.9914645 * jax.random.uniform(splits[9], (SECTIONS, MB, TOPK), jnp.float32) ** levels(splits[9], (SECTIONS, MB, TOPK), ((0, 16),), -0.2, 0.2)), 0.05, 20.0)
    return dict(stream=stream, queries=queries, keyvals=keyvals, w_out=w_out, norm_gain=norm_gain, w_gate=w_gate, w_up=w_up, w_down=w_down, routes=routes, gate_scores=gate_scores)


def reference(stream, queries, keyvals, w_out, norm_gain, w_gate, w_up, w_down, routes, gate_scores):
    heads_here = QHEADS // N_EXPERT
    group = QHEADS // KVHEADS
    scale = 1.0 / math.sqrt(HD)
    query_pos = CTX - MB + jnp.arange(MB, dtype=jnp.int32)
    visible = jnp.arange(CTX, dtype=jnp.int32)[None, :] <= query_pos[:, None]

    def one_section(operands):
        residual, query_all, context, proj_out, gain, gate_w, up_w, down_w, chosen, scores_in = operands

        def one_head(head):
            start = (head * HD).astype(jnp.int32)
            column = (head // group * (2 * HD)).astype(jnp.int32)
            query = lax.dynamic_slice_in_dim(query_all, start, HD, 1)
            keys = lax.dynamic_slice_in_dim(context, column, HD, 1)
            values = lax.dynamic_slice_in_dim(context, column + HD, HD, 1)
            score = jnp.dot(query, keys.T, preferred_element_type=jnp.float32) * scale
            masked = jnp.where(visible, score, -1e+30)
            top = lax.optimization_barrier(jnp.max(masked, axis=1, keepdims=True))
            weight = jnp.where(visible, jnp.exp(score - top), 0.0)
            total = lax.optimization_barrier(jnp.sum(weight, axis=1))
            summed = jnp.dot(weight.astype(jnp.bfloat16), values, preferred_element_type=jnp.float32)
            return (summed / total[:, None]).astype(jnp.bfloat16)
        heads = lax.map(one_head, jnp.arange(QHEADS, dtype=jnp.int32))
        grouped = heads.reshape(N_EXPERT, heads_here, MB, HD).transpose(0, 2, 1, 3).reshape(N_EXPERT, MB, heads_here * HD)
        proj_grouped = proj_out.reshape(N_EXPERT, heads_here * HD, D)
        head_terms = jnp.einsum('emk,ekd->emd', grouped.astype(jnp.float32), proj_grouped.astype(jnp.float32), precision=lax.Precision.HIGHEST)
        head_terms = lax.optimization_barrier(head_terms.astype(jnp.bfloat16)).astype(jnp.float32)
        middle = residual.astype(jnp.float32) + lax.optimization_barrier(jnp.sum(head_terms, axis=0))
        normed = (middle * lax.rsqrt(lax.optimization_barrier(jnp.mean(middle * middle, axis=1, keepdims=True)) + 1e-06) * gain).astype(jnp.bfloat16)
        gate = jnp.dot(normed, gate_w, preferred_element_type=jnp.float32)
        upper = jnp.dot(normed, up_w, preferred_element_type=jnp.float32)
        activated = (jax.nn.silu(gate) * upper).astype(jnp.bfloat16)
        act_dev = activated.reshape(MB, N_EXPERT, HID_DEV).transpose(1, 0, 2)
        down_dev = down_w.reshape(N_EXPERT, HID_DEV, D)
        slice_out = jnp.einsum('dmh,dhk->dmk', act_dev.astype(jnp.float32), down_dev.astype(jnp.float32), precision=lax.Precision.HIGHEST)
        slice_out = lax.optimization_barrier(slice_out.astype(jnp.bfloat16)).astype(jnp.float32)
        onehot = chosen[:, :, None] == jnp.arange(EXPERTS, dtype=jnp.int32)[None, None, :]
        share = lax.optimization_barrier(jnp.sum(jnp.where(onehot, scores_in[:, :, None], 0.0), axis=1)) / lax.optimization_barrier(jnp.sum(scores_in, axis=1, keepdims=True))
        share_dev = jnp.repeat(share, SPLIT, axis=1)
        mixed = jnp.einsum('md,dmk->mk', share_dev, slice_out, precision=lax.Precision.HIGHEST)
        return (middle + mixed).astype(jnp.bfloat16)
    layer_out = lax.map(one_section, (stream, queries, keyvals, w_out, norm_gain, w_gate, w_up, w_down, routes, gate_scores))
    return jnp.roll(layer_out, 1, axis=0)
```

```python
import math

import jax
import jax.numpy as jnp
from jax import lax
from jax.sharding import Mesh
from jax.sharding import PartitionSpec as P

HD = 128
FF = 1536
QHEADS = 32
KVHEADS = 2
CTX = 4096
MB = 256
CAP = 12
EXPERT_AXES = ("y", "zh", "core")


def shifted(block, axis, distance):
    devices = range(lax.axis_size(axis))
    route = [((i - distance) % len(devices), i) for i in devices]
    return lax.ppermute(block, axis, route)


def swap(block, axis):
    return lax.ppermute(block, axis, [(0, 1), (1, 0)])


def body(stream, queries, keyvals, w_out, norm_gain, w_gate, w_up, w_down, routes, gate_scores):
    ny = lax.axis_size("y")
    nz = lax.axis_size("zh")
    nc = lax.axis_size("core")
    yi = lax.axis_index("y")
    zi = lax.axis_index("zh")
    ci = lax.axis_index("core")
    my_index = (yi * nz + zi) * nc + ci
    devices = ny * nz * nc
    tok_rows = stream.shape[1]
    residual = stream[0]
    query_all = queries[0]
    proj_out = w_out[0]
    gain = norm_gain[0]
    gate_w = w_gate[0]
    up_w = w_up[0]
    down_w = w_down[0]
    heads_here = query_all.shape[1] // HD
    group = QHEADS // KVHEADS
    scale = 1.0 / math.sqrt(HD)
    block = keyvals.shape[1]

    kv = keyvals[0].reshape(block, KVHEADS, 2 * HD)
    rows_per_y = nz * nc * heads_here
    head_of_y = [y * rows_per_y // group for y in range(ny)]
    send_kv = jnp.stack([kv[:, h] for h in head_of_y])
    kv_y = lax.all_to_all(send_kv, "y", 0, 0, tiled=True)
    kv_z = jnp.stack([kv_y, swap(kv_y, "zh")])
    kv_c = jnp.stack([kv_z, swap(kv_z, "core")])
    piece = kv_c.reshape(-1, 2 * HD)
    src_c = jnp.where(jnp.arange(2) == 0, ci, 1 - ci)[:, None, None]
    src_z = jnp.where(jnp.arange(2) == 0, zi, 1 - zi)[None, :, None]
    src_y = jnp.arange(ny)[None, None, :]
    src_block = (src_y * nz + src_z) * nc + src_c
    key_pos = (src_block[..., None] * block + jnp.arange(block)[None, None, None, :]).reshape(-1)
    query_pos = CTX - MB + jnp.arange(MB, dtype=jnp.int32)
    visible = key_pos[None, :] <= query_pos[:, None]

    keys = piece[:, :HD]
    values = piece[:, HD:]
    query = query_all.reshape(MB, heads_here, HD).transpose(1, 0, 2)
    score = jnp.einsum("hqd,kd->hqk", query, keys, preferred_element_type=jnp.float32) * scale
    top = jnp.max(jnp.where(visible[None], score, -1e30), axis=2, keepdims=True)
    weight = jnp.where(visible[None], jnp.exp(score - top), 0.0)
    total = jnp.sum(weight, axis=2, keepdims=True)
    summed = jnp.einsum(
        "hqk,kd->hqd", weight.astype(jnp.bfloat16), values, preferred_element_type=jnp.float32
    )
    heads = (summed / total).astype(jnp.bfloat16)
    heads = heads.transpose(1, 0, 2).reshape(MB, heads_here * HD)
    head_terms = jnp.dot(heads, proj_out, preferred_element_type=jnp.float32).astype(jnp.bfloat16)

    terms = head_terms.reshape(ny, nz, nc, tok_rows, -1)
    keep_c = lax.dynamic_index_in_dim(terms, ci, 2, keepdims=False)
    give_c = lax.dynamic_index_in_dim(terms, 1 - ci, 2, keepdims=False)
    part_c = keep_c.astype(jnp.float32) + swap(give_c, "core").astype(jnp.float32)
    part_y = lax.all_to_all(part_c.astype(jnp.bfloat16), "y", 0, 0, tiled=True)
    part_y = jnp.sum(part_y.astype(jnp.float32), axis=0)
    keep_z = lax.dynamic_index_in_dim(part_y, zi, 0, keepdims=False)
    give_z = lax.dynamic_index_in_dim(part_y, 1 - zi, 0, keepdims=False)
    attended = keep_z + swap(give_z.astype(jnp.bfloat16), "zh").astype(jnp.float32)

    middle = residual.astype(jnp.float32) + attended
    normed = (
        middle * lax.rsqrt(jnp.mean(middle * middle, axis=1, keepdims=True) + 1e-06) * gain
    ).astype(jnp.bfloat16)

    split = FF // gate_w.shape[1]
    experts_count = devices // split
    chosen = lax.dynamic_slice_in_dim(routes[0], my_index * tok_rows, tok_rows, 0)
    scores_in = lax.dynamic_slice_in_dim(gate_scores[0], my_index * tok_rows, tok_rows, 0)
    onehot = chosen[:, :, None] == jnp.arange(experts_count, dtype=jnp.int32)[None, None, :]
    share = jnp.sum(jnp.where(onehot, scores_in[:, :, None], 0.0), axis=1) / jnp.sum(
        scores_in, axis=1, keepdims=True
    )
    routed = jnp.any(onehot, axis=1)
    slot = jnp.cumsum(routed.astype(jnp.int32), axis=0) - 1
    select = routed[None] & (slot[None] == jnp.arange(CAP)[:, None, None])
    select = select.transpose(2, 0, 1)
    dispatch = jnp.einsum(
        "xjt,td->xjd", select.astype(jnp.bfloat16), normed, preferred_element_type=jnp.float32
    ).astype(jnp.bfloat16)

    rows_y = lax.all_to_all(dispatch, "y", 0, 0, tiled=True)
    rows_z = jnp.stack([rows_y, swap(rows_y, "zh")])
    rows_c = jnp.stack([rows_z, swap(rows_z, "core")])
    flat = rows_c.reshape(-1, rows_c.shape[-1])
    gate = jnp.dot(flat, gate_w, preferred_element_type=jnp.float32)
    upper = jnp.dot(flat, up_w, preferred_element_type=jnp.float32)
    activated = (jax.nn.silu(gate) * upper).astype(jnp.bfloat16)
    computed = (
        jnp.dot(activated, down_w, preferred_element_type=jnp.float32)
        .astype(jnp.bfloat16)
        .reshape(rows_c.shape)
    )

    back_c = computed[0].astype(jnp.float32) + swap(computed[1], "core").astype(jnp.float32)
    back_c = back_c.astype(jnp.bfloat16)
    back_z = back_c[0].astype(jnp.float32) + swap(back_c[1], "zh").astype(jnp.float32)
    picked = lax.all_to_all(back_z.astype(jnp.bfloat16), "y", 0, 0, tiled=True)
    combine = select.transpose(2, 0, 1).astype(jnp.float32) * share[:, :, None]
    mixed = jnp.einsum(
        "txj,xjd->td", combine, picked.astype(jnp.float32), precision=lax.Precision.HIGHEST
    )
    layer_out = (middle + mixed).astype(jnp.bfloat16)
    return shifted(layer_out[None], "section", 1)


def solution(mesh):
    sizes = (mesh.shape["section"], 4, 2, 2)
    sub = Mesh(mesh.devices.reshape(sizes), ("section",) + EXPERT_AXES)
    ex = EXPERT_AXES
    return jax.shard_map(
        body,
        mesh=sub,
        in_specs=(
            P("section", ex, None),
            P("section", None, ex),
            P("section", ex, None),
            P("section", ex, None),
            P("section", None),
            P("section", None, ex),
            P("section", None, ex),
            P("section", ex, None),
            P("section", None, None),
            P("section", None, None),
        ),
        out_specs=P("section", ex, None),
        check_vma=False,
    )
```

```python
import math

import jax
import jax.numpy as jnp
from jax import lax
from jax.sharding import Mesh
from jax.sharding import PartitionSpec as P

HD = 128
FF = 1536
QHEADS = 32
KVHEADS = 2
CTX = 4096
MB = 256
CAP = 12
EXPERT_AXES = ("y", "zh", "core")


def shifted(block, axis, distance):
    devices = range(lax.axis_size(axis))
    route = [((i - distance) % len(devices), i) for i in devices]
    return lax.ppermute(block, axis, route)


def swap(block, axis):
    return lax.ppermute(block, axis, [(0, 1), (1, 0)])


def body(stream, queries, keyvals, w_out, norm_gain, w_gate, w_up, w_down, routes, gate_scores):
    ny = lax.axis_size("y")
    nz = lax.axis_size("zh")
    nc = lax.axis_size("core")
    yi = lax.axis_index("y")
    zi = lax.axis_index("zh")
    ci = lax.axis_index("core")
    my_index = (yi * nz + zi) * nc + ci
    devices = ny * nz * nc
    tok_rows = stream.shape[1]
    residual = stream[0]
    query_all = queries[0]
    proj_out = w_out[0]
    gain = norm_gain[0]
    gate_w = w_gate[0]
    up_w = w_up[0]
    down_w = w_down[0]
    heads_here = query_all.shape[1] // HD
    group = QHEADS // KVHEADS
    scale = 1.0 / math.sqrt(HD)
    block = keyvals.shape[1]

    kv = keyvals[0].reshape(block, KVHEADS, 2 * HD)
    rows_per_y = nz * nc * heads_here
    head_of_y = [y * rows_per_y // group for y in range(ny)]
    send_kv = jnp.stack([kv[:, h] for h in head_of_y])
    kv_y = lax.all_to_all(send_kv, "y", 0, 0, tiled=True)
    piece = jnp.stack([kv_y, swap(kv_y, "core")]).reshape(-1, 2 * HD)
    src_c = jnp.where(jnp.arange(2) == 0, ci, 1 - ci)[:, None]
    src_y = jnp.arange(ny)[None, :]
    src_block = (src_y * nz + zi) * nc + src_c
    key_pos = (src_block[..., None] * block + jnp.arange(block)[None, None, :]).reshape(-1)
    query_pos = CTX - MB + jnp.arange(MB, dtype=jnp.int32)
    visible = key_pos[None, :] <= query_pos[:, None]

    mine = query_all.reshape(MB, heads_here, HD).transpose(1, 0, 2)
    query = jnp.concatenate([mine, swap(mine, "zh")])
    keys = piece[:, :HD]
    values = piece[:, HD:]
    score = jnp.einsum("hqd,kd->hqk", query, keys, preferred_element_type=jnp.float32) * scale
    top = jnp.max(jnp.where(visible[None], score, -1e30), axis=2, keepdims=True)
    weight = jnp.where(visible[None], jnp.exp(score - top), 0.0)
    total = jnp.sum(weight, axis=2, keepdims=True)
    summed = jnp.einsum(
        "hqk,kd->hqd", weight.astype(jnp.bfloat16), values, preferred_element_type=jnp.float32
    )
    stats = jnp.concatenate([top, total], axis=2)
    far_sum, far_stats = swap(
        (summed[heads_here:].astype(jnp.bfloat16), stats[heads_here:]), "zh"
    )
    near_top = top[:heads_here]
    far_top = far_stats[:, :, 0:1]
    both_top = jnp.maximum(near_top, far_top)
    near_factor = jnp.exp(near_top - both_top)
    far_factor = jnp.exp(far_top - both_top)
    both_total = total[:heads_here] * near_factor + far_stats[:, :, 1:2] * far_factor
    both_sum = summed[:heads_here] * near_factor + far_sum.astype(jnp.float32) * far_factor
    heads = (both_sum / both_total).astype(jnp.bfloat16)
    heads = heads.transpose(1, 0, 2).reshape(MB, heads_here * HD)
    head_terms = jnp.dot(heads, proj_out, preferred_element_type=jnp.float32).astype(jnp.bfloat16)

    terms = head_terms.reshape(ny, nz, nc, tok_rows, -1)
    keep_c = lax.dynamic_index_in_dim(terms, ci, 2, keepdims=False)
    give_c = lax.dynamic_index_in_dim(terms, 1 - ci, 2, keepdims=False)
    part_c = keep_c.astype(jnp.float32) + swap(give_c, "core").astype(jnp.float32)
    part_y = lax.all_to_all(part_c.astype(jnp.bfloat16), "y", 0, 0, tiled=True)
    part_y = jnp.sum(part_y.astype(jnp.float32), axis=0)
    keep_z = lax.dynamic_index_in_dim(part_y, zi, 0, keepdims=False)
    give_z = lax.dynamic_index_in_dim(part_y, 1 - zi, 0, keepdims=False)
    attended = keep_z + swap(give_z.astype(jnp.bfloat16), "zh").astype(jnp.float32)

    middle = residual.astype(jnp.float32) + attended
    normed = (
        middle * lax.rsqrt(jnp.mean(middle * middle, axis=1, keepdims=True) + 1e-06) * gain
    ).astype(jnp.bfloat16)

    split = FF // gate_w.shape[1]
    experts_count = devices // split
    chosen = lax.dynamic_slice_in_dim(routes[0], my_index * tok_rows, tok_rows, 0)
    scores_in = lax.dynamic_slice_in_dim(gate_scores[0], my_index * tok_rows, tok_rows, 0)
    onehot = chosen[:, :, None] == jnp.arange(experts_count, dtype=jnp.int32)[None, None, :]
    share = jnp.sum(jnp.where(onehot, scores_in[:, :, None], 0.0), axis=1) / jnp.sum(
        scores_in, axis=1, keepdims=True
    )
    routed = jnp.any(onehot, axis=1)
    slot = jnp.cumsum(routed.astype(jnp.int32), axis=0) - 1
    select = routed[None] & (slot[None] == jnp.arange(CAP)[:, None, None])
    select = select.transpose(2, 0, 1)
    dispatch = jnp.einsum(
        "xjt,td->xjd", select.astype(jnp.bfloat16), normed, preferred_element_type=jnp.float32
    ).astype(jnp.bfloat16)

    rows_y = lax.all_to_all(dispatch, "y", 0, 0, tiled=True)
    rows_far = swap(rows_y, "zh")
    near = jnp.stack([rows_y, swap(rows_y, "core")])
    far = jnp.stack([rows_far, swap(rows_far, "core")])

    def expert(rows):
        flat = rows.reshape(-1, rows.shape[-1])
        gate = jnp.dot(flat, gate_w, preferred_element_type=jnp.float32)
        upper = jnp.dot(flat, up_w, preferred_element_type=jnp.float32)
        activated = (jax.nn.silu(gate) * upper).astype(jnp.bfloat16)
        out = jnp.dot(activated, down_w, preferred_element_type=jnp.float32)
        return out.astype(jnp.bfloat16).reshape(rows.shape)

    near_out = expert(near)
    far_out = expert(far)

    far_sum = far_out[0].astype(jnp.float32) + swap(far_out[1], "core").astype(jnp.float32)
    near_sum = near_out[0].astype(jnp.float32) + swap(near_out[1], "core").astype(jnp.float32)
    back = near_sum + swap(far_sum.astype(jnp.bfloat16), "zh").astype(jnp.float32)
    picked = lax.all_to_all(back.astype(jnp.bfloat16), "y", 0, 0, tiled=True)
    combine = select.transpose(2, 0, 1).astype(jnp.float32) * share[:, :, None]
    mixed = jnp.einsum(
        "txj,xjd->td", combine, picked.astype(jnp.float32), precision=lax.Precision.HIGHEST
    )
    layer_out = (middle + mixed).astype(jnp.bfloat16)
    return shifted(layer_out[None], "section", 1)


def solution(mesh):
    sizes = (mesh.shape["section"], 4, 2, 2)
    sub = Mesh(mesh.devices.reshape(sizes), ("section",) + EXPERT_AXES)
    ex = EXPERT_AXES
    return jax.shard_map(
        body,
        mesh=sub,
        in_specs=(
            P("section", ex, None),
            P("section", None, ex),
            P("section", ex, None),
            P("section", ex, None),
            P("section", None),
            P("section", None, ex),
            P("section", None, ex),
            P("section", ex, None),
            P("section", None, None),
            P("section", None, None),
        ),
        out_specs=P("section", ex, None),
        check_vma=False,
    )
```

```python
import math

import jax
import jax.numpy as jnp
from jax import lax
from jax.sharding import Mesh
from jax.sharding import PartitionSpec as P

HD = 128
FF = 1536
QHEADS = 32
KVHEADS = 2
CTX = 4096
MB = 256
CAP = 12
EXPERT_AXES = ("y", "zh", "core")


def shifted(block, axis, distance):
    devices = range(lax.axis_size(axis))
    route = [((i - distance) % len(devices), i) for i in devices]
    return lax.ppermute(block, axis, route)


def swap(block, axis):
    return lax.ppermute(block, axis, [(0, 1), (1, 0)])


def body(stream, queries, keyvals, w_out, norm_gain, w_gate, w_up, w_down, routes, gate_scores):
    ny = lax.axis_size("y")
    nz = lax.axis_size("zh")
    nc = lax.axis_size("core")
    yi = lax.axis_index("y")
    zi = lax.axis_index("zh")
    ci = lax.axis_index("core")
    my_index = (yi * nz + zi) * nc + ci
    devices = ny * nz * nc
    tok_rows = stream.shape[1]
    residual = stream[0]
    query_all = queries[0]
    proj_out = w_out[0]
    gain = norm_gain[0]
    gate_w = w_gate[0]
    up_w = w_up[0]
    down_w = w_down[0]
    heads_here = query_all.shape[1] // HD
    group = QHEADS // KVHEADS
    scale = 1.0 / math.sqrt(HD)
    block = keyvals.shape[1]

    kv = keyvals[0].reshape(block, KVHEADS, 2 * HD)
    rows_per_y = nz * nc * heads_here
    head_of_y = [y * rows_per_y // group for y in range(ny)]
    send_kv = jnp.stack([kv[:, h] for h in head_of_y])
    kv_y = lax.all_to_all(send_kv, "y", 0, 0, tiled=True)
    piece = jnp.stack([kv_y, swap(kv_y, "core")]).reshape(-1, 2 * HD)
    src_c = jnp.where(jnp.arange(2) == 0, ci, 1 - ci)[:, None]
    src_y = jnp.arange(ny)[None, :]
    src_block = (src_y * nz + zi) * nc + src_c
    key_pos = (src_block[..., None] * block + jnp.arange(block)[None, None, :]).reshape(-1)
    query_pos = CTX - MB + jnp.arange(MB, dtype=jnp.int32)
    visible = key_pos[None, :] <= query_pos[:, None]

    mine = query_all.reshape(MB, heads_here, HD).transpose(1, 0, 2)
    query = jnp.concatenate([mine, swap(mine, "zh")])
    keys = piece[:, :HD]
    values = piece[:, HD:]
    score = jnp.einsum("hqd,kd->hqk", query, keys, preferred_element_type=jnp.float32) * scale
    top = jnp.max(jnp.where(visible[None], score, -1e30), axis=2, keepdims=True)
    weight = jnp.where(visible[None], jnp.exp(score - top), 0.0)
    total = jnp.sum(weight, axis=2, keepdims=True)
    summed = jnp.einsum(
        "hqk,kd->hqd", weight.astype(jnp.bfloat16), values, preferred_element_type=jnp.float32
    )
    stats = jnp.concatenate([top, total], axis=2)
    far_sum, far_stats = swap(
        (summed[heads_here:].astype(jnp.bfloat16), stats[heads_here:]), "zh"
    )
    near_top = top[:heads_here]
    far_top = far_stats[:, :, 0:1]
    both_top = jnp.maximum(near_top, far_top)
    near_factor = jnp.exp(near_top - both_top)
    far_factor = jnp.exp(far_top - both_top)
    both_total = total[:heads_here] * near_factor + far_stats[:, :, 1:2] * far_factor
    both_sum = summed[:heads_here] * near_factor + far_sum.astype(jnp.float32) * far_factor
    heads = (both_sum / both_total).astype(jnp.bfloat16)
    heads = heads.transpose(1, 0, 2).reshape(MB, heads_here * HD)
    head_terms = jnp.dot(heads, proj_out, preferred_element_type=jnp.float32).astype(jnp.bfloat16)

    terms = head_terms.reshape(ny, nz, nc, tok_rows, -1)
    keep_c = lax.dynamic_index_in_dim(terms, ci, 2, keepdims=False)
    give_c = lax.dynamic_index_in_dim(terms, 1 - ci, 2, keepdims=False)
    part_c = keep_c.astype(jnp.float32) + swap(give_c, "core").astype(jnp.float32)
    part_y = lax.all_to_all(part_c.astype(jnp.bfloat16), "y", 0, 0, tiled=True)
    part_y = jnp.sum(part_y.astype(jnp.float32), axis=0)
    keep_z = lax.dynamic_index_in_dim(part_y, zi, 0, keepdims=False)
    give_z = lax.dynamic_index_in_dim(part_y, 1 - zi, 0, keepdims=False)
    attended = keep_z + swap(give_z.astype(jnp.bfloat16), "zh").astype(jnp.float32)

    middle = residual.astype(jnp.float32) + attended
    normed = (
        middle * lax.rsqrt(jnp.mean(middle * middle, axis=1, keepdims=True) + 1e-06) * gain
    ).astype(jnp.bfloat16)

    split = FF // gate_w.shape[1]
    experts_count = devices // split
    chosen = lax.dynamic_slice_in_dim(routes[0], my_index * tok_rows, tok_rows, 0)
    scores_in = lax.dynamic_slice_in_dim(gate_scores[0], my_index * tok_rows, tok_rows, 0)
    onehot = chosen[:, :, None] == jnp.arange(experts_count, dtype=jnp.int32)[None, None, :]
    share = jnp.sum(jnp.where(onehot, scores_in[:, :, None], 0.0), axis=1) / jnp.sum(
        scores_in, axis=1, keepdims=True
    )
    routed = jnp.any(onehot, axis=1)
    slot = jnp.cumsum(routed.astype(jnp.int32), axis=0) - 1
    select = routed[None] & (slot[None] == jnp.arange(CAP)[:, None, None])
    select = select.transpose(2, 0, 1).reshape(experts_count * CAP, tok_rows)
    dispatch = jnp.dot(
        select.astype(jnp.bfloat16), normed, preferred_element_type=jnp.float32
    ).astype(jnp.bfloat16)

    rows_y = lax.all_to_all(dispatch, "y", 0, 0, tiled=True)
    rows_far = swap(rows_y, "zh")
    near = jnp.concatenate([rows_y, swap(rows_y, "core")])
    far = jnp.concatenate([rows_far, swap(rows_far, "core")])
    count = rows_y.shape[0]

    def expert(rows):
        gate = jnp.dot(rows, gate_w, preferred_element_type=jnp.float32)
        upper = jnp.dot(rows, up_w, preferred_element_type=jnp.float32)
        activated = (jax.nn.silu(gate) * upper).astype(jnp.bfloat16)
        out = jnp.dot(activated, down_w, preferred_element_type=jnp.float32)
        return out.astype(jnp.bfloat16)

    near_out = expert(near)
    far_out = expert(far)

    far_sum = far_out[:count].astype(jnp.float32) + swap(far_out[count:], "core").astype(jnp.float32)
    near_sum = near_out[:count].astype(jnp.float32) + swap(near_out[count:], "core").astype(
        jnp.float32
    )
    back = near_sum + swap(far_sum.astype(jnp.bfloat16), "zh").astype(jnp.float32)
    picked = lax.all_to_all(back.astype(jnp.bfloat16), "y", 0, 0, tiled=True)
    combine = select.T.astype(jnp.float32) * jnp.repeat(share, CAP, axis=1)
    mixed = jnp.dot(combine, picked.astype(jnp.float32), precision=lax.Precision.HIGHEST)
    layer_out = (middle + mixed).astype(jnp.bfloat16)
    return shifted(layer_out[None], "section", 1)


def solution(mesh):
    sizes = (mesh.shape["section"], 4, 2, 2)
    sub = Mesh(mesh.devices.reshape(sizes), ("section",) + EXPERT_AXES)
    ex = EXPERT_AXES
    return jax.shard_map(
        body,
        mesh=sub,
        in_specs=(
            P("section", ex, None),
            P("section", None, ex),
            P("section", ex, None),
            P("section", ex, None),
            P("section", None),
            P("section", None, ex),
            P("section", None, ex),
            P("section", ex, None),
            P("section", None, None),
            P("section", None, None),
        ),
        out_specs=P("section", ex, None),
        check_vma=False,
    )
```

```python
import math

import jax
import jax.numpy as jnp
from jax import lax
from jax.sharding import Mesh
from jax.sharding import PartitionSpec as P

HD = 128
FF = 1536
QHEADS = 32
KVHEADS = 2
CTX = 4096
MB = 256
CAP = 12
EXPERT_AXES = ("y", "zh", "core")


def shifted(block, axis, distance):
    devices = range(lax.axis_size(axis))
    route = [((i - distance) % len(devices), i) for i in devices]
    return lax.ppermute(block, axis, route)


def swap(block, axis):
    return lax.ppermute(block, axis, [(0, 1), (1, 0)])


def body(stream, queries, keyvals, w_out, norm_gain, w_gate, w_up, w_down, routes, gate_scores):
    ny = lax.axis_size("y")
    nz = lax.axis_size("zh")
    nc = lax.axis_size("core")
    yi = lax.axis_index("y")
    zi = lax.axis_index("zh")
    ci = lax.axis_index("core")
    my_index = (yi * nz + zi) * nc + ci
    devices = ny * nz * nc
    tok_rows = stream.shape[1]
    residual = stream[0]
    query_all = queries[0]
    proj_out = w_out[0]
    gain = norm_gain[0]
    gate_w = w_gate[0]
    up_w = w_up[0]
    down_w = w_down[0]
    heads_here = query_all.shape[1] // HD
    group = QHEADS // KVHEADS
    scale = 1.0 / math.sqrt(HD)
    block = keyvals.shape[1]

    kv = keyvals[0].reshape(block, KVHEADS, 2 * HD)
    rows_per_y = nz * nc * heads_here
    head_of_y = [y * rows_per_y // group for y in range(ny)]
    send_kv = jnp.stack([kv[:, h] for h in head_of_y])
    kv_y = lax.all_to_all(send_kv, "y", 0, 0, tiled=True)
    piece = jnp.stack([kv_y, swap(kv_y, "core")]).reshape(-1, 2 * HD)
    src_c = jnp.where(jnp.arange(2) == 0, ci, 1 - ci)[:, None]
    src_y = jnp.arange(ny)[None, :]
    src_block = (src_y * nz + zi) * nc + src_c
    key_pos = (src_block[..., None] * block + jnp.arange(block)[None, None, :]).reshape(-1)
    query_pos = CTX - MB + jnp.arange(MB, dtype=jnp.int32)
    visible = key_pos[None, :] <= query_pos[:, None]

    mine = query_all.reshape(MB, heads_here, HD).transpose(1, 0, 2)
    query = jnp.concatenate([mine, swap(mine, "zh")])
    keys = piece[:, :HD]
    values = piece[:, HD:]
    score = jnp.einsum("hqd,kd->hqk", query, keys, preferred_element_type=jnp.float32) * scale
    top = jnp.max(jnp.where(visible[None], score, -1e30), axis=2, keepdims=True)
    weight = jnp.where(visible[None], jnp.exp(score - top), 0.0)
    total = jnp.sum(weight, axis=2, keepdims=True)
    summed = jnp.einsum(
        "hqk,kd->hqd", weight.astype(jnp.bfloat16), values, preferred_element_type=jnp.float32
    )
    stats = jnp.concatenate([top, total], axis=2)
    far_sum, far_stats = swap(
        (summed[heads_here:].astype(jnp.bfloat16), stats[heads_here:]), "zh"
    )
    near_top = top[:heads_here]
    far_top = far_stats[:, :, 0:1]
    both_top = jnp.maximum(near_top, far_top)
    near_factor = jnp.exp(near_top - both_top)
    far_factor = jnp.exp(far_top - both_top)
    both_total = total[:heads_here] * near_factor + far_stats[:, :, 1:2] * far_factor
    both_sum = summed[:heads_here] * near_factor + far_sum.astype(jnp.float32) * far_factor
    heads = (both_sum / both_total).astype(jnp.bfloat16)
    heads = heads.transpose(1, 0, 2).reshape(MB, heads_here * HD)
    head_terms = jnp.dot(heads, proj_out, preferred_element_type=jnp.float32).astype(jnp.bfloat16)

    terms = head_terms.reshape(ny, nz, nc, tok_rows, -1)
    keep_c = lax.dynamic_index_in_dim(terms, ci, 2, keepdims=False)
    give_c = lax.dynamic_index_in_dim(terms, 1 - ci, 2, keepdims=False)
    part_c = keep_c.astype(jnp.float32) + swap(give_c, "core").astype(jnp.float32)
    part_y = lax.all_to_all(part_c.astype(jnp.bfloat16), "y", 0, 0, tiled=True)
    part_y = jnp.sum(part_y.astype(jnp.float32), axis=0)
    keep_z = lax.dynamic_index_in_dim(part_y, zi, 0, keepdims=False)
    give_z = lax.dynamic_index_in_dim(part_y, 1 - zi, 0, keepdims=False)
    attended = keep_z + swap(give_z.astype(jnp.bfloat16), "zh").astype(jnp.float32)

    middle = residual.astype(jnp.float32) + attended
    normed = (
        middle * lax.rsqrt(jnp.mean(middle * middle, axis=1, keepdims=True) + 1e-06) * gain
    ).astype(jnp.bfloat16)

    split = FF // gate_w.shape[1]
    experts_count = devices // split
    partner = (yi * nz + (1 - zi)) * nc + ci

    def plan(owner):
        chosen = lax.dynamic_slice_in_dim(routes[0], owner * tok_rows, tok_rows, 0)
        scores_in = lax.dynamic_slice_in_dim(gate_scores[0], owner * tok_rows, tok_rows, 0)
        onehot = chosen[:, :, None] == jnp.arange(experts_count, dtype=jnp.int32)[None, None, :]
        share = jnp.sum(jnp.where(onehot, scores_in[:, :, None], 0.0), axis=1) / jnp.sum(
            scores_in, axis=1, keepdims=True
        )
        routed = jnp.any(onehot, axis=1)
        slot = jnp.cumsum(routed.astype(jnp.int32), axis=0) - 1
        select = routed[None] & (slot[None] == jnp.arange(CAP)[:, None, None])
        select = select.transpose(2, 0, 1).reshape(experts_count * CAP, tok_rows)
        combine = select.T.astype(jnp.float32) * jnp.repeat(share, CAP, axis=1)
        return select.astype(jnp.bfloat16), combine

    normed_far = swap(normed, "zh")
    select_own, combine_own = plan(my_index)
    select_far, combine_far = plan(partner)
    dispatch_own = jnp.dot(select_own, normed, preferred_element_type=jnp.float32)
    dispatch_far = jnp.dot(select_far, normed_far, preferred_element_type=jnp.float32)
    rows_own = lax.all_to_all(dispatch_own.astype(jnp.bfloat16), "y", 0, 0, tiled=True)
    rows_far = lax.all_to_all(dispatch_far.astype(jnp.bfloat16), "y", 0, 0, tiled=True)
    near = jnp.concatenate([rows_own, swap(rows_own, "core")])
    far = jnp.concatenate([rows_far, swap(rows_far, "core")])
    count = rows_own.shape[0]

    def expert(rows):
        gate = jnp.dot(rows, gate_w, preferred_element_type=jnp.float32)
        upper = jnp.dot(rows, up_w, preferred_element_type=jnp.float32)
        activated = (jax.nn.silu(gate) * upper).astype(jnp.bfloat16)
        out = jnp.dot(activated, down_w, preferred_element_type=jnp.float32)
        return out.astype(jnp.bfloat16)

    near_out = expert(near)
    far_out = expert(far)

    far_sum = far_out[:count].astype(jnp.float32) + swap(far_out[count:], "core").astype(jnp.float32)
    near_sum = near_out[:count].astype(jnp.float32) + swap(near_out[count:], "core").astype(
        jnp.float32
    )
    back_far = lax.all_to_all(far_sum.astype(jnp.bfloat16), "y", 0, 0, tiled=True)
    back_own = lax.all_to_all(near_sum.astype(jnp.bfloat16), "y", 0, 0, tiled=True)
    hi = lax.Precision.HIGHEST
    mixed_far = jnp.dot(combine_far, back_far.astype(jnp.float32), precision=hi)
    mixed_own = jnp.dot(combine_own, back_own.astype(jnp.float32), precision=hi)
    mixed = mixed_own + swap(mixed_far.astype(jnp.bfloat16), "zh").astype(jnp.float32)
    layer_out = (middle + mixed).astype(jnp.bfloat16)
    return shifted(layer_out[None], "section", 1)


def solution(mesh):
    sizes = (mesh.shape["section"], 4, 2, 2)
    sub = Mesh(mesh.devices.reshape(sizes), ("section",) + EXPERT_AXES)
    ex = EXPERT_AXES
    return jax.shard_map(
        body,
        mesh=sub,
        in_specs=(
            P("section", ex, None),
            P("section", None, ex),
            P("section", ex, None),
            P("section", ex, None),
            P("section", None),
            P("section", None, ex),
            P("section", None, ex),
            P("section", ex, None),
            P("section", None, None),
            P("section", None, None),
        ),
        out_specs=P("section", ex, None),
        check_vma=False,
    )
```

```python
import math

import jax
import jax.numpy as jnp
from jax import lax
from jax.sharding import Mesh
from jax.sharding import PartitionSpec as P

HD = 128
FF = 1536
QHEADS = 32
KVHEADS = 2
CTX = 4096
MB = 256
CAP = 12
EXPERT_AXES = ("y", "zh", "core")


def shifted(block, axis, distance):
    devices = range(lax.axis_size(axis))
    route = [((i - distance) % len(devices), i) for i in devices]
    return lax.ppermute(block, axis, route)


def swap(block, axis):
    return lax.ppermute(block, axis, [(0, 1), (1, 0)])


def body(stream, queries, keyvals, w_out, norm_gain, w_gate, w_up, w_down, routes, gate_scores):
    ny = lax.axis_size("y")
    nz = lax.axis_size("zh")
    nc = lax.axis_size("core")
    yi = lax.axis_index("y")
    zi = lax.axis_index("zh")
    ci = lax.axis_index("core")
    my_index = (yi * nz + zi) * nc + ci
    devices = ny * nz * nc
    tok_rows = stream.shape[1]
    residual = stream[0]
    query_all = queries[0]
    proj_out = w_out[0]
    gain = norm_gain[0]
    gate_w = w_gate[0]
    up_w = w_up[0]
    down_w = w_down[0]
    heads_here = query_all.shape[1] // HD
    group = QHEADS // KVHEADS
    scale = 1.0 / math.sqrt(HD)
    block = keyvals.shape[1]

    kv = keyvals[0].reshape(block, KVHEADS, 2 * HD)
    rows_per_y = nz * nc * heads_here
    head_of_y = [y * rows_per_y // group for y in range(ny)]
    send_kv = jnp.stack([kv[:, h] for h in head_of_y])
    kv_y = lax.all_to_all(send_kv, "y", 0, 0, tiled=True)
    piece = jnp.stack([kv_y, swap(kv_y, "core")]).reshape(-1, 2 * HD)
    src_c = jnp.where(jnp.arange(2) == 0, ci, 1 - ci)[:, None]
    src_y = jnp.arange(ny)[None, :]
    src_block = (src_y * nz + zi) * nc + src_c
    key_pos = (src_block[..., None] * block + jnp.arange(block)[None, None, :]).reshape(-1)
    query_pos = CTX - MB + jnp.arange(MB, dtype=jnp.int32)
    visible = key_pos[None, :] <= query_pos[:, None]

    mine = query_all.reshape(MB, heads_here, HD).transpose(1, 0, 2)
    query = jnp.concatenate([mine, swap(mine, "zh")])
    keys = piece[:, :HD]
    values = piece[:, HD:]
    score = jnp.einsum("hqd,kd->hqk", query, keys, preferred_element_type=jnp.float32) * scale
    top = jnp.max(jnp.where(visible[None], score, -1e30), axis=2, keepdims=True)
    weight = jnp.where(visible[None], jnp.exp(score - top), 0.0)
    total = jnp.sum(weight, axis=2, keepdims=True)
    summed = jnp.einsum(
        "hqk,kd->hqd", weight.astype(jnp.bfloat16), values, preferred_element_type=jnp.float32
    )
    stats = jnp.concatenate([top, total], axis=2)
    far_sum, far_stats = swap(
        (summed[heads_here:].astype(jnp.bfloat16), stats[heads_here:]), "zh"
    )
    near_top = top[:heads_here]
    far_top = far_stats[:, :, 0:1]
    both_top = jnp.maximum(near_top, far_top)
    near_factor = jnp.exp(near_top - both_top)
    far_factor = jnp.exp(far_top - both_top)
    both_total = total[:heads_here] * near_factor + far_stats[:, :, 1:2] * far_factor
    both_sum = summed[:heads_here] * near_factor + far_sum.astype(jnp.float32) * far_factor
    heads = (both_sum / both_total).astype(jnp.bfloat16)
    heads = heads.transpose(1, 0, 2).reshape(MB, heads_here * HD)
    head_terms = jnp.dot(heads, proj_out, preferred_element_type=jnp.float32).astype(jnp.bfloat16)

    terms = head_terms.reshape(ny, nz, nc, tok_rows, -1)
    keep_c = lax.dynamic_index_in_dim(terms, ci, 2, keepdims=False)
    give_c = lax.dynamic_index_in_dim(terms, 1 - ci, 2, keepdims=False)
    part_c = keep_c.astype(jnp.float32) + swap(give_c, "core").astype(jnp.float32)
    part_y = lax.all_to_all(part_c.astype(jnp.bfloat16), "y", 0, 0, tiled=True)
    part_y = jnp.sum(part_y.astype(jnp.float32), axis=0)
    keep_z = lax.dynamic_index_in_dim(part_y, zi, 0, keepdims=False)
    give_z = lax.dynamic_index_in_dim(part_y, 1 - zi, 0, keepdims=False)
    attended = keep_z + swap(give_z.astype(jnp.bfloat16), "zh").astype(jnp.float32)

    middle = residual.astype(jnp.float32) + attended
    normed = (
        middle * lax.rsqrt(jnp.mean(middle * middle, axis=1, keepdims=True) + 1e-06) * gain
    ).astype(jnp.bfloat16)

    split = FF // gate_w.shape[1]
    experts_count = devices // split
    partner = (yi * nz + (1 - zi)) * nc + ci

    def plan(owner):
        chosen = lax.dynamic_slice_in_dim(routes[0], owner * tok_rows, tok_rows, 0)
        scores_in = lax.dynamic_slice_in_dim(gate_scores[0], owner * tok_rows, tok_rows, 0)
        onehot = chosen[:, :, None] == jnp.arange(experts_count, dtype=jnp.int32)[None, None, :]
        share = jnp.sum(jnp.where(onehot, scores_in[:, :, None], 0.0), axis=1) / jnp.sum(
            scores_in, axis=1, keepdims=True
        )
        routed = jnp.any(onehot, axis=1)
        slot = jnp.cumsum(routed.astype(jnp.int32), axis=0) - 1
        select = routed[None] & (slot[None] == jnp.arange(CAP)[:, None, None])
        select = select.transpose(2, 0, 1).reshape(experts_count * CAP, tok_rows)
        combine = select.T.astype(jnp.float32) * jnp.repeat(share, CAP, axis=1)
        return select.astype(jnp.bfloat16), combine

    normed_far = swap(normed, "zh")
    select_own, combine_own = plan(my_index)
    select_far, combine_far = plan(partner)
    dispatch_own = jnp.dot(select_own, normed, preferred_element_type=jnp.float32)
    dispatch_far = jnp.dot(select_far, normed_far, preferred_element_type=jnp.float32)
    width = normed.shape[1]
    dispatch = jnp.stack(
        [dispatch_own.reshape(experts_count, CAP, width), dispatch_far.reshape(experts_count, CAP, width)],
        axis=1,
    ).astype(jnp.bfloat16)
    rows_y = lax.all_to_all(dispatch, "y", 0, 0, tiled=True)
    rows = jnp.stack([rows_y, swap(rows_y, "core")])
    flat = rows.reshape(-1, width)
    gate = jnp.dot(flat, gate_w, preferred_element_type=jnp.float32)
    upper = jnp.dot(flat, up_w, preferred_element_type=jnp.float32)
    activated = (jax.nn.silu(gate) * upper).astype(jnp.bfloat16)
    computed = (
        jnp.dot(activated, down_w, preferred_element_type=jnp.float32)
        .astype(jnp.bfloat16)
        .reshape(rows.shape)
    )

    chip_sum = computed[0].astype(jnp.float32) + swap(computed[1], "core").astype(jnp.float32)
    back = lax.all_to_all(chip_sum.astype(jnp.bfloat16), "y", 0, 0, tiled=True).astype(jnp.float32)
    hi = lax.Precision.HIGHEST
    combine_own = combine_own.reshape(tok_rows, experts_count, CAP)
    combine_far = combine_far.reshape(tok_rows, experts_count, CAP)
    mixed_own = jnp.einsum("txj,xjd->td", combine_own, back[:, 0], precision=hi)
    mixed_far = jnp.einsum("txj,xjd->td", combine_far, back[:, 1], precision=hi)
    mixed = mixed_own + swap(mixed_far.astype(jnp.bfloat16), "zh").astype(jnp.float32)
    layer_out = (middle + mixed).astype(jnp.bfloat16)
    return shifted(layer_out[None], "section", 1)


def solution(mesh):
    sizes = (mesh.shape["section"], 4, 2, 2)
    sub = Mesh(mesh.devices.reshape(sizes), ("section",) + EXPERT_AXES)
    ex = EXPERT_AXES
    return jax.shard_map(
        body,
        mesh=sub,
        in_specs=(
            P("section", ex, None),
            P("section", None, ex),
            P("section", ex, None),
            P("section", ex, None),
            P("section", None),
            P("section", None, ex),
            P("section", None, ex),
            P("section", ex, None),
            P("section", None, None),
            P("section", None, None),
        ),
        out_specs=P("section", ex, None),
        check_vma=False,
    )
```

```python
import math

import jax
import jax.numpy as jnp
from jax import lax
from jax.sharding import Mesh
from jax.sharding import PartitionSpec as P

HD = 128
FF = 1536
QHEADS = 32
KVHEADS = 2
CTX = 4096
MB = 256
CAP = 16
EXPERT_AXES = ("y", "zh", "core")


def shifted(block, axis, distance):
    devices = range(lax.axis_size(axis))
    route = [((i - distance) % len(devices), i) for i in devices]
    return lax.ppermute(block, axis, route)


def swap(block, axis):
    return lax.ppermute(block, axis, [(0, 1), (1, 0)])


def body(stream, queries, keyvals, w_out, norm_gain, w_gate, w_up, w_down, routes, gate_scores):
    ny = lax.axis_size("y")
    nz = lax.axis_size("zh")
    nc = lax.axis_size("core")
    yi = lax.axis_index("y")
    zi = lax.axis_index("zh")
    ci = lax.axis_index("core")
    my_index = (yi * nz + zi) * nc + ci
    devices = ny * nz * nc
    tok_rows = stream.shape[1]
    residual = stream[0]
    query_all = queries[0]
    proj_out = w_out[0]
    gain = norm_gain[0]
    gate_w = w_gate[0]
    up_w = w_up[0]
    down_w = w_down[0]
    heads_here = query_all.shape[1] // HD
    group = QHEADS // KVHEADS
    scale = 1.0 / math.sqrt(HD)
    block = keyvals.shape[1]

    kv = keyvals[0].reshape(block, KVHEADS, 2 * HD)
    rows_per_y = nz * nc * heads_here
    head_of_y = [y * rows_per_y // group for y in range(ny)]
    send_kv = jnp.stack([kv[:, h] for h in head_of_y])
    kv_y = lax.all_to_all(send_kv, "y", 0, 0, tiled=True)
    piece = jnp.stack([kv_y, swap(kv_y, "core")]).reshape(-1, 2 * HD)
    src_c = jnp.where(jnp.arange(2) == 0, ci, 1 - ci)[:, None]
    src_y = jnp.arange(ny)[None, :]
    src_block = (src_y * nz + zi) * nc + src_c
    key_pos = (src_block[..., None] * block + jnp.arange(block)[None, None, :]).reshape(-1)
    query_pos = CTX - MB + jnp.arange(MB, dtype=jnp.int32)
    visible = key_pos[None, :] <= query_pos[:, None]

    mine = query_all.reshape(MB, heads_here, HD).transpose(1, 0, 2)
    query = jnp.concatenate([mine, swap(mine, "zh")])
    keys = piece[:, :HD]
    values = piece[:, HD:]
    score = jnp.einsum("hqd,kd->hqk", query, keys, preferred_element_type=jnp.float32) * scale
    top = jnp.max(jnp.where(visible[None], score, -1e30), axis=2, keepdims=True)
    weight = jnp.where(visible[None], jnp.exp(score - top), 0.0)
    total = jnp.sum(weight, axis=2, keepdims=True)
    summed = jnp.einsum(
        "hqk,kd->hqd", weight.astype(jnp.bfloat16), values, preferred_element_type=jnp.float32
    )
    stats = jnp.concatenate([top, total], axis=2)
    far_sum, far_stats = swap(
        (summed[heads_here:].astype(jnp.bfloat16), stats[heads_here:]), "zh"
    )
    near_top = top[:heads_here]
    far_top = far_stats[:, :, 0:1]
    both_top = jnp.maximum(near_top, far_top)
    near_factor = jnp.exp(near_top - both_top)
    far_factor = jnp.exp(far_top - both_top)
    both_total = total[:heads_here] * near_factor + far_stats[:, :, 1:2] * far_factor
    both_sum = summed[:heads_here] * near_factor + far_sum.astype(jnp.float32) * far_factor
    heads = (both_sum / both_total).astype(jnp.bfloat16)
    heads = heads.transpose(1, 0, 2).reshape(MB, heads_here * HD)
    head_terms = jnp.dot(heads, proj_out, preferred_element_type=jnp.float32).astype(jnp.bfloat16)

    terms = head_terms.reshape(ny, nz, nc, tok_rows, -1)
    keep_c = lax.dynamic_index_in_dim(terms, ci, 2, keepdims=False)
    give_c = lax.dynamic_index_in_dim(terms, 1 - ci, 2, keepdims=False)
    part_c = keep_c.astype(jnp.float32) + swap(give_c, "core").astype(jnp.float32)
    part_y = lax.all_to_all(part_c.astype(jnp.bfloat16), "y", 0, 0, tiled=True)
    part_y = jnp.sum(part_y.astype(jnp.float32), axis=0)
    keep_z = lax.dynamic_index_in_dim(part_y, zi, 0, keepdims=False)
    give_z = lax.dynamic_index_in_dim(part_y, 1 - zi, 0, keepdims=False)
    attended = keep_z + swap(give_z.astype(jnp.bfloat16), "zh").astype(jnp.float32)

    middle = residual.astype(jnp.float32) + attended
    normed = (
        middle * lax.rsqrt(jnp.mean(middle * middle, axis=1, keepdims=True) + 1e-06) * gain
    ).astype(jnp.bfloat16)

    split = FF // gate_w.shape[1]
    experts_count = devices // split
    partner = (yi * nz + (1 - zi)) * nc + ci

    def plan(owner):
        chosen = lax.dynamic_slice_in_dim(routes[0], owner * tok_rows, tok_rows, 0)
        scores_in = lax.dynamic_slice_in_dim(gate_scores[0], owner * tok_rows, tok_rows, 0)
        onehot = chosen[:, :, None] == jnp.arange(experts_count, dtype=jnp.int32)[None, None, :]
        share = jnp.sum(jnp.where(onehot, scores_in[:, :, None], 0.0), axis=1) / jnp.sum(
            scores_in, axis=1, keepdims=True
        )
        routed = jnp.any(onehot, axis=1)
        slot = jnp.cumsum(routed.astype(jnp.int32), axis=0) - 1
        select = routed[None] & (slot[None] == jnp.arange(CAP)[:, None, None])
        select = select.transpose(2, 0, 1).reshape(experts_count * CAP, tok_rows)
        combine = select.T.astype(jnp.float32) * jnp.repeat(share, CAP, axis=1)
        return select.astype(jnp.bfloat16), combine

    normed_far = swap(normed, "zh")
    select_own, combine_own = plan(my_index)
    select_far, combine_far = plan(partner)
    dispatch_own = jnp.dot(select_own, normed, preferred_element_type=jnp.float32)
    dispatch_far = jnp.dot(select_far, normed_far, preferred_element_type=jnp.float32)
    width = normed.shape[1]
    dispatch = jnp.stack(
        [dispatch_own.reshape(experts_count, CAP, width), dispatch_far.reshape(experts_count, CAP, width)],
        axis=1,
    ).astype(jnp.bfloat16)
    rows_y = lax.all_to_all(dispatch, "y", 0, 0, tiled=True)
    rows = jnp.stack([rows_y, swap(rows_y, "core")])
    flat = rows.reshape(-1, width)
    gate = jnp.dot(flat, gate_w, preferred_element_type=jnp.float32)
    upper = jnp.dot(flat, up_w, preferred_element_type=jnp.float32)
    activated = (jax.nn.silu(gate) * upper).astype(jnp.bfloat16)
    computed = (
        jnp.dot(activated, down_w, preferred_element_type=jnp.float32)
        .astype(jnp.bfloat16)
        .reshape(rows.shape)
    )

    chip_sum = computed[0].astype(jnp.float32) + swap(computed[1], "core").astype(jnp.float32)
    back = lax.all_to_all(chip_sum.astype(jnp.bfloat16), "y", 0, 0, tiled=True).astype(jnp.float32)
    hi = lax.Precision.HIGHEST
    combine_own = combine_own.reshape(tok_rows, experts_count, CAP)
    combine_far = combine_far.reshape(tok_rows, experts_count, CAP)
    mixed_own = jnp.einsum("txj,xjd->td", combine_own, back[:, 0], precision=hi)
    mixed_far = jnp.einsum("txj,xjd->td", combine_far, back[:, 1], precision=hi)
    mixed = mixed_own + swap(mixed_far.astype(jnp.bfloat16), "zh").astype(jnp.float32)
    layer_out = (middle + mixed).astype(jnp.bfloat16)
    return shifted(layer_out[None], "section", 1)


def solution(mesh):
    sizes = (mesh.shape["section"], 4, 2, 2)
    sub = Mesh(mesh.devices.reshape(sizes), ("section",) + EXPERT_AXES)
    ex = EXPERT_AXES
    return jax.shard_map(
        body,
        mesh=sub,
        in_specs=(
            P("section", ex, None),
            P("section", None, ex),
            P("section", ex, None),
            P("section", ex, None),
            P("section", None),
            P("section", None, ex),
            P("section", None, ex),
            P("section", ex, None),
            P("section", None, None),
            P("section", None, None),
        ),
        out_specs=P("section", ex, None),
        check_vma=False,
    )
```

```python
import math

import jax
import jax.numpy as jnp
from jax import lax
from jax.sharding import Mesh
from jax.sharding import PartitionSpec as P

HD = 128
FF = 1536
QHEADS = 32
KVHEADS = 2
CTX = 4096
MB = 256
CAP = 16
EXPERT_AXES = ("y", "zh", "core")


def shifted(block, axis, distance):
    devices = range(lax.axis_size(axis))
    route = [((i - distance) % len(devices), i) for i in devices]
    return lax.ppermute(block, axis, route)


def swap(block, axis):
    return lax.ppermute(block, axis, [(0, 1), (1, 0)])


def body(stream, queries, keyvals, w_out, norm_gain, w_gate, w_up, w_down, routes, gate_scores):
    ny = lax.axis_size("y")
    nz = lax.axis_size("zh")
    nc = lax.axis_size("core")
    yi = lax.axis_index("y")
    zi = lax.axis_index("zh")
    ci = lax.axis_index("core")
    my_index = (yi * nz + zi) * nc + ci
    devices = ny * nz * nc
    tok_rows = stream.shape[1]
    residual = stream[0]
    query_all = queries[0]
    proj_out = w_out[0]
    gain = norm_gain[0]
    gate_w = w_gate[0]
    up_w = w_up[0]
    down_w = w_down[0]
    heads_here = query_all.shape[1] // HD
    group = QHEADS // KVHEADS
    scale = 1.0 / math.sqrt(HD)
    block = keyvals.shape[1]

    kv = keyvals[0].reshape(block, KVHEADS, 2 * HD)
    rows_per_y = nz * nc * heads_here
    head_of_y = [y * rows_per_y // group for y in range(ny)]
    send_kv = jnp.stack([kv[:, h] for h in head_of_y])
    kv_y = lax.all_to_all(send_kv, "y", 0, 0, tiled=True)
    piece = jnp.stack([kv_y, swap(kv_y, "core")]).reshape(-1, 2 * HD)
    src_c = jnp.where(jnp.arange(2) == 0, ci, 1 - ci)[:, None]
    src_y = jnp.arange(ny)[None, :]
    src_block = (src_y * nz + zi) * nc + src_c
    key_pos = (src_block[..., None] * block + jnp.arange(block)[None, None, :]).reshape(-1)
    query_pos = CTX - MB + jnp.arange(MB, dtype=jnp.int32)
    visible = key_pos[None, :] <= query_pos[:, None]

    mine = query_all.reshape(MB, heads_here, HD).transpose(1, 0, 2)
    keys = piece[:, :HD]
    values = piece[:, HD:]

    def partial(query):
        score = jnp.einsum("hqd,kd->hqk", query, keys, preferred_element_type=jnp.float32) * scale
        top = jnp.max(jnp.where(visible[None], score, -1e30), axis=2, keepdims=True)
        weight = jnp.where(visible[None], jnp.exp(score - top), 0.0)
        total = jnp.sum(weight, axis=2, keepdims=True)
        summed = jnp.einsum(
            "hqk,kd->hqd", weight.astype(jnp.bfloat16), values, preferred_element_type=jnp.float32
        )
        return summed, top, total

    other_sum, other_top, other_total = partial(swap(mine, "zh"))
    far_sum, far_stats = swap(
        (other_sum.astype(jnp.bfloat16), jnp.concatenate([other_top, other_total], axis=2)), "zh"
    )
    near_sum, near_top, near_total = partial(mine)
    far_top = far_stats[:, :, 0:1]
    both_top = jnp.maximum(near_top, far_top)
    near_factor = jnp.exp(near_top - both_top)
    far_factor = jnp.exp(far_top - both_top)
    both_total = near_total * near_factor + far_stats[:, :, 1:2] * far_factor
    both_sum = near_sum * near_factor + far_sum.astype(jnp.float32) * far_factor
    heads = (both_sum / both_total).astype(jnp.bfloat16)
    heads = heads.transpose(1, 0, 2).reshape(MB, heads_here * HD)
    head_terms = jnp.dot(heads, proj_out, preferred_element_type=jnp.float32).astype(jnp.bfloat16)

    terms = head_terms.reshape(ny, nz, nc, tok_rows, -1)
    keep_c = lax.dynamic_index_in_dim(terms, ci, 2, keepdims=False)
    give_c = lax.dynamic_index_in_dim(terms, 1 - ci, 2, keepdims=False)
    part_c = keep_c.astype(jnp.float32) + swap(give_c, "core").astype(jnp.float32)
    part_y = lax.all_to_all(part_c.astype(jnp.bfloat16), "y", 0, 0, tiled=True)
    part_y = jnp.sum(part_y.astype(jnp.float32), axis=0)
    keep_z = lax.dynamic_index_in_dim(part_y, zi, 0, keepdims=False)
    give_z = lax.dynamic_index_in_dim(part_y, 1 - zi, 0, keepdims=False)
    attended = keep_z + swap(give_z.astype(jnp.bfloat16), "zh").astype(jnp.float32)

    middle = residual.astype(jnp.float32) + attended
    normed = (
        middle * lax.rsqrt(jnp.mean(middle * middle, axis=1, keepdims=True) + 1e-06) * gain
    ).astype(jnp.bfloat16)

    split = FF // gate_w.shape[1]
    experts_count = devices // split
    partner = (yi * nz + (1 - zi)) * nc + ci

    def plan(owner):
        chosen = lax.dynamic_slice_in_dim(routes[0], owner * tok_rows, tok_rows, 0)
        scores_in = lax.dynamic_slice_in_dim(gate_scores[0], owner * tok_rows, tok_rows, 0)
        onehot = chosen[:, :, None] == jnp.arange(experts_count, dtype=jnp.int32)[None, None, :]
        share = jnp.sum(jnp.where(onehot, scores_in[:, :, None], 0.0), axis=1) / jnp.sum(
            scores_in, axis=1, keepdims=True
        )
        routed = jnp.any(onehot, axis=1)
        slot = jnp.cumsum(routed.astype(jnp.int32), axis=0) - 1
        select = routed[None] & (slot[None] == jnp.arange(CAP)[:, None, None])
        select = select.transpose(2, 0, 1).reshape(experts_count * CAP, tok_rows)
        combine = select.T.astype(jnp.float32) * jnp.repeat(share, CAP, axis=1)
        return select.astype(jnp.bfloat16), combine

    normed_far = swap(normed, "zh")
    select_own, combine_own = plan(my_index)
    select_far, combine_far = plan(partner)
    dispatch_own = jnp.dot(select_own, normed, preferred_element_type=jnp.float32)
    dispatch_far = jnp.dot(select_far, normed_far, preferred_element_type=jnp.float32)
    width = normed.shape[1]
    dispatch = jnp.stack(
        [dispatch_own.reshape(experts_count, CAP, width), dispatch_far.reshape(experts_count, CAP, width)],
        axis=1,
    ).astype(jnp.bfloat16)
    rows_y = lax.all_to_all(dispatch, "y", 0, 0, tiled=True)
    rows = jnp.stack([rows_y, swap(rows_y, "core")])
    flat = rows.reshape(-1, width)
    gate = jnp.dot(flat, gate_w, preferred_element_type=jnp.float32)
    upper = jnp.dot(flat, up_w, preferred_element_type=jnp.float32)
    activated = (jax.nn.silu(gate) * upper).astype(jnp.bfloat16)
    computed = (
        jnp.dot(activated, down_w, preferred_element_type=jnp.float32)
        .astype(jnp.bfloat16)
        .reshape(rows.shape)
    )

    chip_sum = computed[0].astype(jnp.float32) + swap(computed[1], "core").astype(jnp.float32)
    back = lax.all_to_all(chip_sum.astype(jnp.bfloat16), "y", 0, 0, tiled=True).astype(jnp.float32)
    hi = lax.Precision.HIGHEST
    combine_own = combine_own.reshape(tok_rows, experts_count, CAP)
    combine_far = combine_far.reshape(tok_rows, experts_count, CAP)
    mixed_own = jnp.einsum("txj,xjd->td", combine_own, back[:, 0], precision=hi)
    mixed_far = jnp.einsum("txj,xjd->td", combine_far, back[:, 1], precision=hi)
    own_part = shifted((middle + mixed_own).astype(jnp.bfloat16), "section", 1)
    sections = lax.axis_size("section")
    route = [
        (s * nz + z, ((s + 1) % sections) * nz + (nz - 1 - z)) for s in range(sections) for z in range(nz)
    ]
    far_part = lax.ppermute(mixed_far.astype(jnp.bfloat16), ("section", "zh"), route)
    layer_out = own_part.astype(jnp.float32) + far_part.astype(jnp.float32)
    return layer_out.astype(jnp.bfloat16)[None]


def solution(mesh):
    sizes = (mesh.shape["section"], 4, 2, 2)
    sub = Mesh(mesh.devices.reshape(sizes), ("section",) + EXPERT_AXES)
    ex = EXPERT_AXES
    return jax.shard_map(
        body,
        mesh=sub,
        in_specs=(
            P("section", ex, None),
            P("section", None, ex),
            P("section", ex, None),
            P("section", ex, None),
            P("section", None),
            P("section", None, ex),
            P("section", None, ex),
            P("section", ex, None),
            P("section", None, None),
            P("section", None, None),
        ),
        out_specs=P("section", ex, None),
        check_vma=False,
    )
```

```python
import math

import jax
import jax.numpy as jnp
from jax import lax
from jax.sharding import Mesh
from jax.sharding import PartitionSpec as P

HD = 128
FF = 1536
QHEADS = 32
KVHEADS = 2
CTX = 4096
MB = 256
CAP = 16
EXPERT_AXES = ("y", "zh", "core")


def shifted(block, axis, distance):
    devices = range(lax.axis_size(axis))
    route = [((i - distance) % len(devices), i) for i in devices]
    return lax.ppermute(block, axis, route)


def swap(block, axis):
    return lax.ppermute(block, axis, [(0, 1), (1, 0)])


def body(stream, queries, keyvals, w_out, norm_gain, w_gate, w_up, w_down, routes, gate_scores):
    ny = lax.axis_size("y")
    nz = lax.axis_size("zh")
    nc = lax.axis_size("core")
    yi = lax.axis_index("y")
    zi = lax.axis_index("zh")
    ci = lax.axis_index("core")
    my_index = (yi * nz + zi) * nc + ci
    devices = ny * nz * nc
    tok_rows = stream.shape[1]
    residual = stream[0]
    residual_far = swap(residual, "zh")
    query_all = queries[0]
    proj_out = w_out[0]
    gain = norm_gain[0]
    gate_w = w_gate[0]
    up_w = w_up[0]
    down_w = w_down[0]
    heads_here = query_all.shape[1] // HD
    group = QHEADS // KVHEADS
    scale = 1.0 / math.sqrt(HD)
    block = keyvals.shape[1]

    kv = keyvals[0].reshape(block, KVHEADS, 2 * HD)
    rows_per_y = nz * nc * heads_here
    head_of_y = [y * rows_per_y // group for y in range(ny)]
    send_kv = jnp.stack([kv[:, h] for h in head_of_y])
    kv_y = lax.all_to_all(send_kv, "y", 0, 0, tiled=True)
    piece = jnp.stack([kv_y, swap(kv_y, "core")]).reshape(-1, 2 * HD)
    src_c = jnp.where(jnp.arange(2) == 0, ci, 1 - ci)[:, None]
    src_y = jnp.arange(ny)[None, :]
    src_block = (src_y * nz + zi) * nc + src_c
    key_pos = (src_block[..., None] * block + jnp.arange(block)[None, None, :]).reshape(-1)
    query_pos = CTX - MB + jnp.arange(MB, dtype=jnp.int32)
    visible = key_pos[None, :] <= query_pos[:, None]

    mine = query_all.reshape(MB, heads_here, HD).transpose(1, 0, 2)
    keys = piece[:, :HD]
    values = piece[:, HD:]

    def partial(query):
        score = jnp.einsum("hqd,kd->hqk", query, keys, preferred_element_type=jnp.float32) * scale
        top = jnp.max(jnp.where(visible[None], score, -1e30), axis=2, keepdims=True)
        weight = jnp.where(visible[None], jnp.exp(score - top), 0.0)
        total = jnp.sum(weight, axis=2, keepdims=True)
        summed = jnp.einsum(
            "hqk,kd->hqd", weight.astype(jnp.bfloat16), values, preferred_element_type=jnp.float32
        )
        return summed, top, total

    other_sum, other_top, other_total = partial(swap(mine, "zh"))
    far_sum, far_stats = swap(
        (other_sum.astype(jnp.bfloat16), jnp.concatenate([other_top, other_total], axis=2)), "zh"
    )
    near_sum, near_top, near_total = partial(mine)
    far_top = far_stats[:, :, 0:1]
    both_top = jnp.maximum(near_top, far_top)
    near_factor = jnp.exp(near_top - both_top)
    far_factor = jnp.exp(far_top - both_top)
    both_total = near_total * near_factor + far_stats[:, :, 1:2] * far_factor
    both_sum = near_sum * near_factor + far_sum.astype(jnp.float32) * far_factor
    heads = (both_sum / both_total).astype(jnp.bfloat16)
    heads = heads.transpose(1, 0, 2).reshape(MB, heads_here * HD)
    head_terms = jnp.dot(heads, proj_out, preferred_element_type=jnp.float32).astype(jnp.bfloat16)

    terms = head_terms.reshape(ny, nz, nc, tok_rows, -1)
    keep_c = lax.dynamic_index_in_dim(terms, ci, 2, keepdims=False)
    give_c = lax.dynamic_index_in_dim(terms, 1 - ci, 2, keepdims=False)
    part_c = keep_c.astype(jnp.float32) + swap(give_c, "core").astype(jnp.float32)
    part_y = lax.all_to_all(part_c.astype(jnp.bfloat16), "y", 0, 0, tiled=True)
    part_y = jnp.sum(part_y.astype(jnp.float32), axis=0)
    keep_z = lax.dynamic_index_in_dim(part_y, zi, 0, keepdims=False)
    give_z = lax.dynamic_index_in_dim(part_y, 1 - zi, 0, keepdims=False)
    got = swap(jnp.stack([give_z, keep_z]).astype(jnp.bfloat16), "zh").astype(jnp.float32)
    attended = keep_z.astype(jnp.bfloat16).astype(jnp.float32) + got[0]
    attended_far = give_z.astype(jnp.bfloat16).astype(jnp.float32) + got[1]

    def norm(middle):
        return (
            middle * lax.rsqrt(jnp.mean(middle * middle, axis=1, keepdims=True) + 1e-06) * gain
        ).astype(jnp.bfloat16)

    middle = residual.astype(jnp.float32) + attended
    normed = norm(middle)
    normed_far = norm(residual_far.astype(jnp.float32) + attended_far)

    split = FF // gate_w.shape[1]
    experts_count = devices // split
    partner = (yi * nz + (1 - zi)) * nc + ci

    def plan(owner):
        chosen = lax.dynamic_slice_in_dim(routes[0], owner * tok_rows, tok_rows, 0)
        scores_in = lax.dynamic_slice_in_dim(gate_scores[0], owner * tok_rows, tok_rows, 0)
        onehot = chosen[:, :, None] == jnp.arange(experts_count, dtype=jnp.int32)[None, None, :]
        share = jnp.sum(jnp.where(onehot, scores_in[:, :, None], 0.0), axis=1) / jnp.sum(
            scores_in, axis=1, keepdims=True
        )
        routed = jnp.any(onehot, axis=1)
        slot = jnp.cumsum(routed.astype(jnp.int32), axis=0) - 1
        select = routed[None] & (slot[None] == jnp.arange(CAP)[:, None, None])
        select = select.transpose(2, 0, 1).reshape(experts_count * CAP, tok_rows)
        combine = select.T.astype(jnp.float32) * jnp.repeat(share, CAP, axis=1)
        return select.astype(jnp.bfloat16), combine

    select_own, combine_own = plan(my_index)
    select_far, combine_far = plan(partner)
    dispatch_own = jnp.dot(select_own, normed, preferred_element_type=jnp.float32)
    dispatch_far = jnp.dot(select_far, normed_far, preferred_element_type=jnp.float32)
    width = normed.shape[1]
    dispatch = jnp.stack(
        [dispatch_own.reshape(experts_count, CAP, width), dispatch_far.reshape(experts_count, CAP, width)],
        axis=1,
    ).astype(jnp.bfloat16)
    rows_y = lax.all_to_all(dispatch, "y", 0, 0, tiled=True)
    rows = jnp.stack([rows_y, swap(rows_y, "core")])
    flat = rows.reshape(-1, width)
    gate = jnp.dot(flat, gate_w, preferred_element_type=jnp.float32)
    upper = jnp.dot(flat, up_w, preferred_element_type=jnp.float32)
    activated = (jax.nn.silu(gate) * upper).astype(jnp.bfloat16)
    computed = (
        jnp.dot(activated, down_w, preferred_element_type=jnp.float32)
        .astype(jnp.bfloat16)
        .reshape(rows.shape)
    )

    chip_sum = computed[0].astype(jnp.float32) + swap(computed[1], "core").astype(jnp.float32)
    back = lax.all_to_all(chip_sum.astype(jnp.bfloat16), "y", 0, 0, tiled=True).astype(jnp.float32)
    hi = lax.Precision.HIGHEST
    combine_own = combine_own.reshape(tok_rows, experts_count, CAP)
    combine_far = combine_far.reshape(tok_rows, experts_count, CAP)
    mixed_own = jnp.einsum("txj,xjd->td", combine_own, back[:, 0], precision=hi)
    mixed_far = jnp.einsum("txj,xjd->td", combine_far, back[:, 1], precision=hi)
    own_part = shifted((middle + mixed_own).astype(jnp.bfloat16), "section", 1)
    sections = lax.axis_size("section")
    route = [
        (s * nz + z, ((s + 1) % sections) * nz + (nz - 1 - z)) for s in range(sections) for z in range(nz)
    ]
    far_part = lax.ppermute(mixed_far.astype(jnp.bfloat16), ("section", "zh"), route)
    layer_out = own_part.astype(jnp.float32) + far_part.astype(jnp.float32)
    return layer_out.astype(jnp.bfloat16)[None]


def solution(mesh):
    sizes = (mesh.shape["section"], 4, 2, 2)
    sub = Mesh(mesh.devices.reshape(sizes), ("section",) + EXPERT_AXES)
    ex = EXPERT_AXES
    return jax.shard_map(
        body,
        mesh=sub,
        in_specs=(
            P("section", ex, None),
            P("section", None, ex),
            P("section", ex, None),
            P("section", ex, None),
            P("section", None),
            P("section", None, ex),
            P("section", None, ex),
            P("section", ex, None),
            P("section", None, None),
            P("section", None, None),
        ),
        out_specs=P("section", ex, None),
        check_vma=False,
    )
```

```python
import math

import jax
import jax.numpy as jnp
from jax import lax
from jax.sharding import Mesh
from jax.sharding import PartitionSpec as P

HD = 128
FF = 1536
QHEADS = 32
KVHEADS = 2
CTX = 4096
MB = 256
CAP = 16
EXPERT_AXES = ("y", "zh", "core")


def shifted(block, axis, distance):
    devices = range(lax.axis_size(axis))
    route = [((i - distance) % len(devices), i) for i in devices]
    return lax.ppermute(block, axis, route)


def swap(block, axis):
    return lax.ppermute(block, axis, [(0, 1), (1, 0)])


def body(stream, queries, keyvals, w_out, norm_gain, w_gate, w_up, w_down, routes, gate_scores):
    ny = lax.axis_size("y")
    nz = lax.axis_size("zh")
    nc = lax.axis_size("core")
    yi = lax.axis_index("y")
    zi = lax.axis_index("zh")
    ci = lax.axis_index("core")
    my_index = (yi * nz + zi) * nc + ci
    devices = ny * nz * nc
    tok_rows = stream.shape[1]
    residual = stream[0]
    residual_far = swap(residual, "zh")
    query_all = queries[0]
    proj_out = w_out[0]
    gain = norm_gain[0]
    gate_w = w_gate[0]
    up_w = w_up[0]
    down_w = w_down[0]
    heads_here = query_all.shape[1] // HD
    group = QHEADS // KVHEADS
    scale = 1.0 / math.sqrt(HD)
    block = keyvals.shape[1]

    kv = keyvals[0].reshape(block, KVHEADS, 2 * HD)
    rows_per_y = nz * nc * heads_here
    head_of_y = [y * rows_per_y // group for y in range(ny)]
    send_kv = jnp.stack([kv[:, h] for h in head_of_y])
    kv_y = lax.all_to_all(send_kv, "y", 0, 0, tiled=True)
    piece = jnp.stack([kv_y, swap(kv_y, "core")]).reshape(-1, 2 * HD)
    src_c = jnp.where(jnp.arange(2) == 0, ci, 1 - ci)[:, None]
    src_y = jnp.arange(ny)[None, :]
    src_block = (src_y * nz + zi) * nc + src_c
    key_pos = (src_block[..., None] * block + jnp.arange(block)[None, None, :]).reshape(-1)
    query_pos = CTX - MB + jnp.arange(MB, dtype=jnp.int32)
    visible = key_pos[None, :] <= query_pos[:, None]

    mine = query_all.reshape(MB, heads_here, HD).transpose(1, 0, 2)
    keys = piece[:, :HD]
    values = piece[:, HD:]

    def partial(query):
        score = jnp.einsum("hqd,kd->hqk", query, keys, preferred_element_type=jnp.float32) * scale
        top = jnp.max(jnp.where(visible[None], score, -1e30), axis=2, keepdims=True)
        weight = jnp.where(visible[None], jnp.exp(score - top), 0.0)
        total = jnp.sum(weight, axis=2, keepdims=True)
        summed = jnp.einsum(
            "hqk,kd->hqd", weight.astype(jnp.bfloat16), values, preferred_element_type=jnp.float32
        )
        return summed, top, total

    other_sum, other_top, other_total = partial(swap(mine, "zh"))
    far_sum, far_stats = swap(
        (other_sum.astype(jnp.bfloat16), jnp.concatenate([other_top, other_total], axis=2)), "zh"
    )
    near_sum, near_top, near_total = partial(mine)
    far_top = far_stats[:, :, 0:1]
    both_top = jnp.maximum(near_top, far_top)
    near_factor = jnp.exp(near_top - both_top)
    far_factor = jnp.exp(far_top - both_top)
    both_total = near_total * near_factor + far_stats[:, :, 1:2] * far_factor
    both_sum = near_sum * near_factor + far_sum.astype(jnp.float32) * far_factor
    heads = (both_sum / both_total).astype(jnp.bfloat16)
    heads = heads.transpose(1, 0, 2).reshape(MB, heads_here * HD)
    head_terms = jnp.dot(heads, proj_out, preferred_element_type=jnp.float32).astype(jnp.bfloat16)

    terms = head_terms.reshape(ny, nz, nc, tok_rows, -1)
    keep_c = lax.dynamic_index_in_dim(terms, ci, 2, keepdims=False)
    give_c = lax.dynamic_index_in_dim(terms, 1 - ci, 2, keepdims=False)
    part_c = keep_c.astype(jnp.float32) + swap(give_c, "core").astype(jnp.float32)
    part_y = lax.all_to_all(part_c.astype(jnp.bfloat16), "y", 0, 0, tiled=True)
    part_y = jnp.sum(part_y.astype(jnp.float32), axis=0)
    keep_z = lax.dynamic_index_in_dim(part_y, zi, 0, keepdims=False)
    give_z = lax.dynamic_index_in_dim(part_y, 1 - zi, 0, keepdims=False)
    got = swap(jnp.stack([give_z, keep_z]).astype(jnp.bfloat16), "zh").astype(jnp.float32)
    attended = keep_z.astype(jnp.bfloat16).astype(jnp.float32) + got[0]
    attended_far = give_z.astype(jnp.bfloat16).astype(jnp.float32) + got[1]

    def norm(middle):
        return (
            middle * lax.rsqrt(jnp.mean(middle * middle, axis=1, keepdims=True) + 1e-06) * gain
        ).astype(jnp.bfloat16)

    middle = residual.astype(jnp.float32) + attended
    normed = norm(middle)
    normed_far = norm(residual_far.astype(jnp.float32) + attended_far)

    split = FF // gate_w.shape[1]
    experts_count = devices // split
    partner = (yi * nz + (1 - zi)) * nc + ci

    def plan(owner):
        chosen = lax.dynamic_slice_in_dim(routes[0], owner * tok_rows, tok_rows, 0)
        scores_in = lax.dynamic_slice_in_dim(gate_scores[0], owner * tok_rows, tok_rows, 0)
        onehot = chosen[:, :, None] == jnp.arange(experts_count, dtype=jnp.int32)[None, None, :]
        share = jnp.sum(jnp.where(onehot, scores_in[:, :, None], 0.0), axis=1) / jnp.sum(
            scores_in, axis=1, keepdims=True
        )
        routed = jnp.any(onehot, axis=1)
        slot = jnp.cumsum(routed.astype(jnp.int32), axis=0) - 1
        select = routed[None] & (slot[None] == jnp.arange(CAP)[:, None, None])
        select = select.transpose(2, 0, 1).reshape(experts_count * CAP, tok_rows)
        combine = select.T.astype(jnp.float32) * jnp.repeat(share, CAP, axis=1)
        return select.astype(jnp.bfloat16), combine

    select_own, combine_own = plan(my_index)
    select_far, combine_far = plan(partner)
    dispatch_own = jnp.dot(select_own, normed, preferred_element_type=jnp.float32)
    dispatch_far = jnp.dot(select_far, normed_far, preferred_element_type=jnp.float32)
    width = normed.shape[1]
    dispatch = jnp.stack(
        [dispatch_own.reshape(experts_count, CAP, width), dispatch_far.reshape(experts_count, CAP, width)],
        axis=1,
    ).astype(jnp.bfloat16)
    rows_y = lax.all_to_all(dispatch, "y", 0, 0, tiled=True)
    rows = jnp.stack([rows_y, swap(rows_y, "core")])
    flat = rows.reshape(-1, width)
    gate = jnp.dot(flat, gate_w, preferred_element_type=jnp.float32)
    upper = jnp.dot(flat, up_w, preferred_element_type=jnp.float32)
    activated = (jax.nn.silu(gate) * upper).astype(jnp.bfloat16)
    computed = (
        jnp.dot(activated, down_w, preferred_element_type=jnp.float32)
        .astype(jnp.bfloat16)
        .reshape(rows.shape)
    )

    chip_sum = computed[0].astype(jnp.float32) + swap(computed[1], "core").astype(jnp.float32)
    hi = lax.Precision.HIGHEST
    combine_own = combine_own.reshape(tok_rows, experts_count, CAP)
    combine_far = combine_far.reshape(tok_rows, experts_count, CAP)
    back_far = lax.all_to_all(chip_sum[:, 1].astype(jnp.bfloat16), "y", 0, 0, tiled=True)
    mixed_far = jnp.einsum("txj,xjd->td", combine_far, back_far.astype(jnp.float32), precision=hi)
    sections = lax.axis_size("section")
    route = [
        (s * nz + z, ((s + 1) % sections) * nz + (nz - 1 - z)) for s in range(sections) for z in range(nz)
    ]
    far_part = lax.ppermute(mixed_far.astype(jnp.bfloat16), ("section", "zh"), route)
    back_own = lax.all_to_all(chip_sum[:, 0].astype(jnp.bfloat16), "y", 0, 0, tiled=True)
    mixed_own = jnp.einsum("txj,xjd->td", combine_own, back_own.astype(jnp.float32), precision=hi)
    own_part = shifted((middle + mixed_own).astype(jnp.bfloat16), "section", 1)
    layer_out = own_part.astype(jnp.float32) + far_part.astype(jnp.float32)
    return layer_out.astype(jnp.bfloat16)[None]


def solution(mesh):
    sizes = (mesh.shape["section"], 4, 2, 2)
    sub = Mesh(mesh.devices.reshape(sizes), ("section",) + EXPERT_AXES)
    ex = EXPERT_AXES
    return jax.shard_map(
        body,
        mesh=sub,
        in_specs=(
            P("section", ex, None),
            P("section", None, ex),
            P("section", ex, None),
            P("section", ex, None),
            P("section", None),
            P("section", None, ex),
            P("section", None, ex),
            P("section", ex, None),
            P("section", None, None),
            P("section", None, None),
        ),
        out_specs=P("section", ex, None),
        check_vma=False,
    )
```

```python
import math

import jax
import jax.numpy as jnp
from jax import lax
from jax.sharding import Mesh
from jax.sharding import PartitionSpec as P

HD = 128
FF = 1536
QHEADS = 32
KVHEADS = 2
CTX = 4096
MB = 256
CAP = 16
EXPERT_AXES = ("y", "zh", "core")


def shifted(block, axis, distance):
    devices = range(lax.axis_size(axis))
    route = [((i - distance) % len(devices), i) for i in devices]
    return lax.ppermute(block, axis, route)


def swap(block, axis):
    return lax.ppermute(block, axis, [(0, 1), (1, 0)])


def body(stream, queries, keyvals, w_out, norm_gain, w_gate, w_up, w_down, routes, gate_scores):
    ny = lax.axis_size("y")
    nz = lax.axis_size("zh")
    nc = lax.axis_size("core")
    yi = lax.axis_index("y")
    zi = lax.axis_index("zh")
    ci = lax.axis_index("core")
    my_index = (yi * nz + zi) * nc + ci
    devices = ny * nz * nc
    tok_rows = stream.shape[1]
    residual = stream[0]
    residual_far = swap(residual, "zh")
    query_all = queries[0]
    proj_out = w_out[0]
    gain = norm_gain[0]
    gate_w = w_gate[0]
    up_w = w_up[0]
    down_w = w_down[0]
    heads_here = query_all.shape[1] // HD
    group = QHEADS // KVHEADS
    scale = 1.0 / math.sqrt(HD)
    block = keyvals.shape[1]

    kv = keyvals[0].reshape(block, KVHEADS, 2 * HD)
    rows_per_y = nz * nc * heads_here
    head_of_y = [y * rows_per_y // group for y in range(ny)]
    send_kv = jnp.stack([kv[:, h] for h in head_of_y])
    kv_y = lax.all_to_all(send_kv, "y", 0, 0, tiled=True)
    piece = jnp.stack([kv_y, swap(kv_y, "core")]).reshape(-1, 2 * HD)
    src_c = jnp.where(jnp.arange(2) == 0, ci, 1 - ci)[:, None]
    src_y = jnp.arange(ny)[None, :]
    src_block = (src_y * nz + zi) * nc + src_c
    key_pos = (src_block[..., None] * block + jnp.arange(block)[None, None, :]).reshape(-1)
    query_pos = CTX - MB + jnp.arange(MB, dtype=jnp.int32)
    visible = key_pos[None, :] <= query_pos[:, None]

    mine = query_all.reshape(MB, heads_here, HD).transpose(1, 0, 2)
    keys = piece[:, :HD]
    values = piece[:, HD:]

    def partial(query):
        score = jnp.einsum("hqd,kd->hqk", query, keys, preferred_element_type=jnp.float32) * scale
        top = jnp.max(jnp.where(visible[None], score, -1e30), axis=2, keepdims=True)
        weight = jnp.where(visible[None], jnp.exp(score - top), 0.0)
        total = jnp.sum(weight, axis=2, keepdims=True)
        summed = jnp.einsum(
            "hqk,kd->hqd", weight.astype(jnp.bfloat16), values, preferred_element_type=jnp.float32
        )
        return summed, top, total

    other = swap(query_all, "zh").reshape(MB, heads_here, HD).transpose(1, 0, 2)
    other_sum, other_top, other_total = partial(other)
    far_sum, far_stats = swap(
        (other_sum.astype(jnp.bfloat16), jnp.concatenate([other_top, other_total], axis=2)), "zh"
    )
    near_sum, near_top, near_total = partial(mine)
    far_top = far_stats[:, :, 0:1]
    both_top = jnp.maximum(near_top, far_top)
    near_factor = jnp.exp(near_top - both_top)
    far_factor = jnp.exp(far_top - both_top)
    both_total = near_total * near_factor + far_stats[:, :, 1:2] * far_factor
    both_sum = near_sum * near_factor + far_sum.astype(jnp.float32) * far_factor
    heads = (both_sum / both_total).astype(jnp.bfloat16)
    heads = heads.transpose(1, 0, 2).reshape(MB, heads_here * HD)
    head_terms = jnp.dot(heads, proj_out, preferred_element_type=jnp.float32).astype(jnp.bfloat16)

    terms = head_terms.reshape(ny, nz, nc, tok_rows, -1)
    keep_c = lax.dynamic_index_in_dim(terms, ci, 2, keepdims=False)
    give_c = lax.dynamic_index_in_dim(terms, 1 - ci, 2, keepdims=False)
    part_c = keep_c.astype(jnp.float32) + swap(give_c, "core").astype(jnp.float32)
    part_y = lax.all_to_all(part_c.astype(jnp.bfloat16), "y", 0, 0, tiled=True)
    part_y = jnp.sum(part_y.astype(jnp.float32), axis=0)
    keep_z = lax.dynamic_index_in_dim(part_y, zi, 0, keepdims=False)
    give_z = lax.dynamic_index_in_dim(part_y, 1 - zi, 0, keepdims=False)
    got = swap(jnp.stack([give_z, keep_z]).astype(jnp.bfloat16), "zh").astype(jnp.float32)
    attended = keep_z.astype(jnp.bfloat16).astype(jnp.float32) + got[0]
    attended_far = give_z.astype(jnp.bfloat16).astype(jnp.float32) + got[1]

    def norm(middle):
        return (
            middle * lax.rsqrt(jnp.mean(middle * middle, axis=1, keepdims=True) + 1e-06) * gain
        ).astype(jnp.bfloat16)

    middle = residual.astype(jnp.float32) + attended
    normed = norm(middle)
    normed_far = norm(residual_far.astype(jnp.float32) + attended_far)

    split = FF // gate_w.shape[1]
    experts_count = devices // split
    partner = (yi * nz + (1 - zi)) * nc + ci

    def plan(owner):
        chosen = lax.dynamic_slice_in_dim(routes[0], owner * tok_rows, tok_rows, 0)
        scores_in = lax.dynamic_slice_in_dim(gate_scores[0], owner * tok_rows, tok_rows, 0)
        onehot = chosen[:, :, None] == jnp.arange(experts_count, dtype=jnp.int32)[None, None, :]
        share = jnp.sum(jnp.where(onehot, scores_in[:, :, None], 0.0), axis=1) / jnp.sum(
            scores_in, axis=1, keepdims=True
        )
        routed = jnp.any(onehot, axis=1)
        slot = jnp.cumsum(routed.astype(jnp.int32), axis=0) - 1
        select = routed[None] & (slot[None] == jnp.arange(CAP)[:, None, None])
        select = select.transpose(2, 0, 1).reshape(experts_count * CAP, tok_rows)
        combine = select.T.astype(jnp.float32) * jnp.repeat(share, CAP, axis=1)
        return select.astype(jnp.bfloat16), combine

    select_own, combine_own = plan(my_index)
    select_far, combine_far = plan(partner)
    dispatch_own = jnp.dot(select_own, normed, preferred_element_type=jnp.float32)
    dispatch_far = jnp.dot(select_far, normed_far, preferred_element_type=jnp.float32)
    width = normed.shape[1]
    dispatch = jnp.stack(
        [dispatch_own.reshape(experts_count, CAP, width), dispatch_far.reshape(experts_count, CAP, width)],
        axis=1,
    ).astype(jnp.bfloat16)
    rows_y = lax.all_to_all(dispatch, "y", 0, 0, tiled=True)
    rows = jnp.stack([rows_y, swap(rows_y, "core")])
    flat = rows.reshape(-1, width)
    gate = jnp.dot(flat, gate_w, preferred_element_type=jnp.float32)
    upper = jnp.dot(flat, up_w, preferred_element_type=jnp.float32)
    activated = (jax.nn.silu(gate) * upper).astype(jnp.bfloat16)
    computed = (
        jnp.dot(activated, down_w, preferred_element_type=jnp.float32)
        .astype(jnp.bfloat16)
        .reshape(rows.shape)
    )

    chip_sum = computed[0].astype(jnp.float32) + swap(computed[1], "core").astype(jnp.float32)
    back = lax.all_to_all(chip_sum.astype(jnp.bfloat16), "y", 0, 0, tiled=True).astype(jnp.float32)
    hi = lax.Precision.HIGHEST
    combine_own = combine_own.reshape(tok_rows, experts_count, CAP)
    combine_far = combine_far.reshape(tok_rows, experts_count, CAP)
    mixed_own = jnp.einsum("txj,xjd->td", combine_own, back[:, 0], precision=hi)
    mixed_far = jnp.einsum("txj,xjd->td", combine_far, back[:, 1], precision=hi)
    own_part = shifted((middle + mixed_own).astype(jnp.bfloat16), "section", 1)
    sections = lax.axis_size("section")
    route = [
        (s * nz + z, ((s + 1) % sections) * nz + (nz - 1 - z)) for s in range(sections) for z in range(nz)
    ]
    far_part = lax.ppermute(mixed_far.astype(jnp.bfloat16), ("section", "zh"), route)
    layer_out = own_part.astype(jnp.float32) + far_part.astype(jnp.float32)
    return layer_out.astype(jnp.bfloat16)[None]


def solution(mesh):
    sizes = (mesh.shape["section"], 4, 2, 2)
    sub = Mesh(mesh.devices.reshape(sizes), ("section",) + EXPERT_AXES)
    ex = EXPERT_AXES
    return jax.shard_map(
        body,
        mesh=sub,
        in_specs=(
            P("section", ex, None),
            P("section", None, ex),
            P("section", ex, None),
            P("section", ex, None),
            P("section", None),
            P("section", None, ex),
            P("section", None, ex),
            P("section", ex, None),
            P("section", None, None),
            P("section", None, None),
        ),
        out_specs=P("section", ex, None),
        check_vma=False,
    )
```

```python
import math

import jax
import jax.numpy as jnp
from jax import lax
from jax.sharding import Mesh
from jax.sharding import PartitionSpec as P

HD = 128
FF = 1536
QHEADS = 32
KVHEADS = 2
CTX = 4096
MB = 256
CAP = 16
EXPERT_AXES = ("y", "zh", "core")


def shifted(block, axis, distance):
    devices = range(lax.axis_size(axis))
    route = [((i - distance) % len(devices), i) for i in devices]
    return lax.ppermute(block, axis, route)


def swap(block, axis):
    return lax.ppermute(block, axis, [(0, 1), (1, 0)])


def body(stream, queries, keyvals, w_out, norm_gain, w_gate, w_up, w_down, routes, gate_scores):
    ny = lax.axis_size("y")
    nz = lax.axis_size("zh")
    nc = lax.axis_size("core")
    yi = lax.axis_index("y")
    zi = lax.axis_index("zh")
    ci = lax.axis_index("core")
    my_index = (yi * nz + zi) * nc + ci
    devices = ny * nz * nc
    tok_rows = stream.shape[1]
    residual = stream[0]
    residual_far = swap(residual, "zh")
    query_all = queries[0]
    proj_out = w_out[0]
    gain = norm_gain[0]
    gate_w = w_gate[0]
    up_w = w_up[0]
    down_w = w_down[0]
    heads_here = query_all.shape[1] // HD
    group = QHEADS // KVHEADS
    scale = 1.0 / math.sqrt(HD)
    block = keyvals.shape[1]

    kv = keyvals[0].reshape(block, KVHEADS, 2 * HD)
    rows_per_y = nz * nc * heads_here
    head_of_y = [y * rows_per_y // group for y in range(ny)]
    send_kv = jnp.stack([kv[:, h] for h in head_of_y])
    kv_y = lax.all_to_all(send_kv, "y", 0, 0, tiled=True)
    piece = jnp.stack([kv_y, swap(kv_y, "core")]).reshape(-1, 2 * HD)
    src_c = jnp.where(jnp.arange(2) == 0, ci, 1 - ci)[:, None]
    src_y = jnp.arange(ny)[None, :]
    src_block = (src_y * nz + zi) * nc + src_c
    key_pos = (src_block[..., None] * block + jnp.arange(block)[None, None, :]).reshape(-1)
    query_pos = CTX - MB + jnp.arange(MB, dtype=jnp.int32)
    visible = key_pos[None, :] <= query_pos[:, None]

    mine = query_all.reshape(MB, heads_here, HD).transpose(1, 0, 2)
    keys = piece[:, :HD]
    values = piece[:, HD:]

    def partial(query):
        score = jnp.einsum("hqd,kd->hqk", query, keys, preferred_element_type=jnp.float32) * scale
        top = jnp.max(jnp.where(visible[None], score, -1e30), axis=2, keepdims=True)
        weight = jnp.where(visible[None], jnp.exp(score - top), 0.0)
        total = jnp.sum(weight, axis=2, keepdims=True)
        summed = jnp.einsum(
            "hqk,kd->hqd", weight.astype(jnp.bfloat16), values, preferred_element_type=jnp.float32
        )
        return summed, top, total

    other_sum, other_top, other_total = partial(swap(mine, "zh"))
    far_sum, far_stats = swap(
        (other_sum.astype(jnp.bfloat16), jnp.concatenate([other_top, other_total], axis=2)), "zh"
    )
    near_sum, near_top, near_total = partial(mine)
    far_top = far_stats[:, :, 0:1]
    both_top = jnp.maximum(near_top, far_top)
    near_factor = jnp.exp(near_top - both_top)
    far_factor = jnp.exp(far_top - both_top)
    both_total = near_total * near_factor + far_stats[:, :, 1:2] * far_factor
    both_sum = near_sum * near_factor + far_sum.astype(jnp.float32) * far_factor
    heads = (both_sum / both_total).astype(jnp.bfloat16)
    heads = heads.transpose(1, 0, 2).reshape(MB, heads_here * HD)
    head_terms = jnp.dot(heads, proj_out, preferred_element_type=jnp.float32).astype(jnp.bfloat16)

    terms = head_terms.reshape(ny, nz, nc, tok_rows, -1)
    keep_c = lax.dynamic_index_in_dim(terms, ci, 2, keepdims=False)
    give_c = lax.dynamic_index_in_dim(terms, 1 - ci, 2, keepdims=False)
    part_c = keep_c.astype(jnp.float32) + swap(give_c, "core").astype(jnp.float32)
    part_y = lax.all_to_all(part_c.astype(jnp.bfloat16), "y", 0, 0, tiled=True)
    part_y = jnp.sum(part_y.astype(jnp.float32), axis=0)
    keep_z = lax.dynamic_index_in_dim(part_y, zi, 0, keepdims=False)
    give_z = lax.dynamic_index_in_dim(part_y, 1 - zi, 0, keepdims=False)
    got = swap(jnp.stack([give_z, keep_z]).astype(jnp.bfloat16), "zh").astype(jnp.float32)
    attended = keep_z.astype(jnp.bfloat16).astype(jnp.float32) + got[0]
    attended_far = give_z.astype(jnp.bfloat16).astype(jnp.float32) + got[1]

    def norm(middle):
        return (
            middle * lax.rsqrt(jnp.mean(middle * middle, axis=1, keepdims=True) + 1e-06) * gain
        ).astype(jnp.bfloat16)

    middle = residual.astype(jnp.float32) + attended
    normed = norm(middle)
    normed_far = norm(residual_far.astype(jnp.float32) + attended_far)

    split = FF // gate_w.shape[1]
    experts_count = devices // split
    partner = (yi * nz + (1 - zi)) * nc + ci

    def plan(owner):
        chosen = lax.dynamic_slice_in_dim(routes[0], owner * tok_rows, tok_rows, 0)
        scores_in = lax.dynamic_slice_in_dim(gate_scores[0], owner * tok_rows, tok_rows, 0)
        onehot = chosen[:, :, None] == jnp.arange(experts_count, dtype=jnp.int32)[None, None, :]
        share = jnp.sum(jnp.where(onehot, scores_in[:, :, None], 0.0), axis=1) / jnp.sum(
            scores_in, axis=1, keepdims=True
        )
        routed = jnp.any(onehot, axis=1)
        slot = jnp.cumsum(routed.astype(jnp.int32), axis=0) - 1
        select = routed[None] & (slot[None] == jnp.arange(CAP)[:, None, None])
        select = select.transpose(2, 0, 1).reshape(experts_count * CAP, tok_rows)
        combine = select.T.astype(jnp.float32) * jnp.repeat(share, CAP, axis=1)
        return select.astype(jnp.bfloat16), combine

    select_own, combine_own = plan(my_index)
    select_far, combine_far = plan(partner)
    dispatch_own = jnp.dot(select_own, normed, preferred_element_type=jnp.float32)
    dispatch_far = jnp.dot(select_far, normed_far, preferred_element_type=jnp.float32)
    width = normed.shape[1]
    dispatch = jnp.stack(
        [dispatch_own.reshape(experts_count, CAP, width), dispatch_far.reshape(experts_count, CAP, width)],
        axis=1,
    ).astype(jnp.bfloat16)
    rows_y = lax.all_to_all(dispatch, "y", 0, 0, tiled=True)
    rows = jnp.stack([rows_y, swap(rows_y, "core")])
    flat = rows.reshape(-1, width)
    gate = jnp.dot(flat, gate_w, preferred_element_type=jnp.float32)
    upper = jnp.dot(flat, up_w, preferred_element_type=jnp.float32)
    activated = lax.optimization_barrier((jax.nn.silu(gate) * upper).astype(jnp.bfloat16))
    computed = (
        jnp.dot(activated, down_w, preferred_element_type=jnp.float32)
        .astype(jnp.bfloat16)
        .reshape(rows.shape)
    )

    chip_sum = computed[0].astype(jnp.float32) + swap(computed[1], "core").astype(jnp.float32)
    back = lax.all_to_all(chip_sum.astype(jnp.bfloat16), "y", 0, 0, tiled=True).astype(jnp.float32)
    hi = lax.Precision.HIGHEST
    combine_own = combine_own.reshape(tok_rows, experts_count, CAP)
    combine_far = combine_far.reshape(tok_rows, experts_count, CAP)
    mixed_own = jnp.einsum("txj,xjd->td", combine_own, back[:, 0], precision=hi)
    mixed_far = jnp.einsum("txj,xjd->td", combine_far, back[:, 1], precision=hi)
    own_part = shifted((middle + mixed_own).astype(jnp.bfloat16), "section", 1)
    sections = lax.axis_size("section")
    route = [
        (s * nz + z, ((s + 1) % sections) * nz + (nz - 1 - z)) for s in range(sections) for z in range(nz)
    ]
    far_part = lax.ppermute(mixed_far.astype(jnp.bfloat16), ("section", "zh"), route)
    layer_out = own_part.astype(jnp.float32) + far_part.astype(jnp.float32)
    return layer_out.astype(jnp.bfloat16)[None]


def solution(mesh):
    sizes = (mesh.shape["section"], 4, 2, 2)
    sub = Mesh(mesh.devices.reshape(sizes), ("section",) + EXPERT_AXES)
    ex = EXPERT_AXES
    return jax.shard_map(
        body,
        mesh=sub,
        in_specs=(
            P("section", ex, None),
            P("section", None, ex),
            P("section", ex, None),
            P("section", ex, None),
            P("section", None),
            P("section", None, ex),
            P("section", None, ex),
            P("section", ex, None),
            P("section", None, None),
            P("section", None, None),
        ),
        out_specs=P("section", ex, None),
        check_vma=False,
    )
```

```python
import math

import jax
import jax.numpy as jnp
from jax import lax
from jax.sharding import Mesh
from jax.sharding import PartitionSpec as P

HD = 128
FF = 1536
QHEADS = 32
KVHEADS = 2
CTX = 4096
MB = 256
CAP = 16
EXPERT_AXES = ("y", "zh", "core")


def shifted(block, axis, distance):
    devices = range(lax.axis_size(axis))
    route = [((i - distance) % len(devices), i) for i in devices]
    return lax.ppermute(block, axis, route)


def swap(block, axis):
    return lax.ppermute(block, axis, [(0, 1), (1, 0)])


def body(stream, queries, keyvals, w_out, norm_gain, w_gate, w_up, w_down, routes, gate_scores):
    ny = lax.axis_size("y")
    nz = lax.axis_size("zh")
    nc = lax.axis_size("core")
    yi = lax.axis_index("y")
    zi = lax.axis_index("zh")
    ci = lax.axis_index("core")
    my_index = (yi * nz + zi) * nc + ci
    devices = ny * nz * nc
    tok_rows = stream.shape[1]
    residual = stream[0]
    residual_far = swap(residual, "zh")
    query_all = queries[0]
    proj_out = w_out[0]
    gain = norm_gain[0]
    gate_w = w_gate[0]
    up_w = w_up[0]
    down_w = w_down[0]
    heads_here = query_all.shape[1] // HD
    group = QHEADS // KVHEADS
    scale = 1.0 / math.sqrt(HD)
    block = keyvals.shape[1]

    kv = keyvals[0].reshape(block, KVHEADS, 2 * HD)
    rows_per_y = nz * nc * heads_here
    head_of_y = [y * rows_per_y // group for y in range(ny)]
    send_kv = jnp.stack([kv[:, h] for h in head_of_y])
    kv_y = lax.all_to_all(send_kv, "y", 0, 0, tiled=True)
    piece = jnp.stack([kv_y, swap(kv_y, "core")]).reshape(-1, 2 * HD)
    src_c = jnp.where(jnp.arange(2) == 0, ci, 1 - ci)[:, None]
    src_y = jnp.arange(ny)[None, :]
    src_block = (src_y * nz + zi) * nc + src_c
    key_pos = (src_block[..., None] * block + jnp.arange(block)[None, None, :]).reshape(-1)
    query_pos = CTX - MB + jnp.arange(MB, dtype=jnp.int32)
    visible = key_pos[None, :] <= query_pos[:, None]

    mine = query_all.reshape(MB, heads_here, HD).transpose(1, 0, 2)
    keys = piece[:, :HD]
    values = piece[:, HD:]

    def partial(query):
        score = jnp.einsum("hqd,kd->hqk", query, keys, preferred_element_type=jnp.float32) * scale
        top = jnp.max(jnp.where(visible[None], score, -1e30), axis=2, keepdims=True)
        weight = jnp.where(visible[None], jnp.exp(score - top), 0.0)
        total = jnp.sum(weight, axis=2, keepdims=True)
        summed = jnp.einsum(
            "hqk,kd->hqd", weight.astype(jnp.bfloat16), values, preferred_element_type=jnp.float32
        )
        return summed, top, total

    other_sum, other_top, other_total = partial(swap(mine, "zh"))
    far_sum, far_stats = swap(
        (other_sum.astype(jnp.bfloat16), jnp.concatenate([other_top, other_total], axis=2)), "zh"
    )
    near_sum, near_top, near_total = partial(mine)
    far_top = far_stats[:, :, 0:1]
    both_top = jnp.maximum(near_top, far_top)
    near_factor = jnp.exp(near_top - both_top)
    far_factor = jnp.exp(far_top - both_top)
    both_total = near_total * near_factor + far_stats[:, :, 1:2] * far_factor
    both_sum = near_sum * near_factor + far_sum.astype(jnp.float32) * far_factor
    heads = (both_sum / both_total).astype(jnp.bfloat16)
    heads = heads.transpose(1, 0, 2).reshape(MB, heads_here * HD)
    head_terms = jnp.dot(heads, proj_out, preferred_element_type=jnp.float32).astype(jnp.bfloat16)

    terms = head_terms.reshape(ny, nz, nc, tok_rows, -1)
    keep_c = lax.dynamic_index_in_dim(terms, ci, 2, keepdims=False)
    give_c = lax.dynamic_index_in_dim(terms, 1 - ci, 2, keepdims=False)
    part_c = keep_c.astype(jnp.float32) + swap(give_c, "core").astype(jnp.float32)
    part_y = lax.all_to_all(part_c.astype(jnp.bfloat16), "y", 0, 0, tiled=True)
    part_y = jnp.sum(part_y.astype(jnp.float32), axis=0)
    keep_z = lax.dynamic_index_in_dim(part_y, zi, 0, keepdims=False)
    give_z = lax.dynamic_index_in_dim(part_y, 1 - zi, 0, keepdims=False)
    got = swap(jnp.stack([give_z, keep_z]).astype(jnp.bfloat16), "zh").astype(jnp.float32)
    attended = keep_z.astype(jnp.bfloat16).astype(jnp.float32) + got[0]
    attended_far = give_z.astype(jnp.bfloat16).astype(jnp.float32) + got[1]

    def norm(middle):
        return (
            middle * lax.rsqrt(jnp.mean(middle * middle, axis=1, keepdims=True) + 1e-06) * gain
        ).astype(jnp.bfloat16)

    middle = residual.astype(jnp.float32) + attended
    normed = norm(middle)
    normed_far = norm(residual_far.astype(jnp.float32) + attended_far)

    split = FF // gate_w.shape[1]
    experts_count = devices // split
    partner = (yi * nz + (1 - zi)) * nc + ci

    def plan(owner):
        chosen = lax.dynamic_slice_in_dim(routes[0], owner * tok_rows, tok_rows, 0)
        scores_in = lax.dynamic_slice_in_dim(gate_scores[0], owner * tok_rows, tok_rows, 0)
        onehot = chosen[:, :, None] == jnp.arange(experts_count, dtype=jnp.int32)[None, None, :]
        share = jnp.sum(jnp.where(onehot, scores_in[:, :, None], 0.0), axis=1) / jnp.sum(
            scores_in, axis=1, keepdims=True
        )
        routed = jnp.any(onehot, axis=1)
        slot = jnp.cumsum(routed.astype(jnp.int32), axis=0) - 1
        select = routed[None] & (slot[None] == jnp.arange(CAP)[:, None, None])
        select = select.transpose(2, 0, 1).reshape(experts_count * CAP, tok_rows)
        combine = select.T.astype(jnp.float32) * jnp.repeat(share, CAP, axis=1)
        return select.astype(jnp.bfloat16), combine

    select_own, combine_own = plan(my_index)
    select_far, combine_far = plan(partner)
    dispatch_own = jnp.dot(select_own, normed, preferred_element_type=jnp.float32)
    dispatch_far = jnp.dot(select_far, normed_far, preferred_element_type=jnp.float32)
    width = normed.shape[1]
    dispatch = jnp.stack(
        [dispatch_own.reshape(experts_count, CAP, width), dispatch_far.reshape(experts_count, CAP, width)],
        axis=1,
    ).astype(jnp.bfloat16)
    rows_y = lax.all_to_all(dispatch, "y", 0, 0, tiled=True)
    rows = jnp.stack([rows_y, swap(rows_y, "core")])
    flat = rows.reshape(-1, width)
    gate = jnp.dot(flat, gate_w, preferred_element_type=jnp.float32)
    upper = jnp.dot(flat, up_w, preferred_element_type=jnp.float32)
    activated = lax.optimization_barrier((jax.nn.silu(gate) * upper).astype(jnp.bfloat16))
    computed = (
        jnp.dot(activated, down_w, preferred_element_type=jnp.float32)
        .astype(jnp.bfloat16)
        .reshape(rows.shape)
    )

    chip_sum = computed[0].astype(jnp.float32) + swap(computed[1], "core").astype(jnp.float32)
    back = lax.all_to_all(chip_sum.astype(jnp.bfloat16), "y", 0, 0, tiled=True)

    def mix(combine, outs):
        combine = combine.reshape(tok_rows, experts_count, CAP)
        high = combine.astype(jnp.bfloat16)
        low = (combine - high.astype(jnp.float32)).astype(jnp.bfloat16)
        return sum(
            jnp.einsum("txj,xjd->td", part, outs, preferred_element_type=jnp.float32)
            for part in (high, low)
        )

    mixed_own = mix(combine_own, back[:, 0])
    mixed_far = mix(combine_far, back[:, 1])
    own_part = shifted((middle + mixed_own).astype(jnp.bfloat16), "section", 1)
    sections = lax.axis_size("section")
    route = [
        (s * nz + z, ((s + 1) % sections) * nz + (nz - 1 - z)) for s in range(sections) for z in range(nz)
    ]
    far_part = lax.ppermute(mixed_far.astype(jnp.bfloat16), ("section", "zh"), route)
    layer_out = own_part.astype(jnp.float32) + far_part.astype(jnp.float32)
    return layer_out.astype(jnp.bfloat16)[None]


def solution(mesh):
    sizes = (mesh.shape["section"], 4, 2, 2)
    sub = Mesh(mesh.devices.reshape(sizes), ("section",) + EXPERT_AXES)
    ex = EXPERT_AXES
    return jax.shard_map(
        body,
        mesh=sub,
        in_specs=(
            P("section", ex, None),
            P("section", None, ex),
            P("section", ex, None),
            P("section", ex, None),
            P("section", None),
            P("section", None, ex),
            P("section", None, ex),
            P("section", ex, None),
            P("section", None, None),
            P("section", None, None),
        ),
        out_specs=P("section", ex, None),
        check_vma=False,
    )
```

```python
import math

import jax
import jax.numpy as jnp
from jax import lax
from jax.sharding import Mesh
from jax.sharding import PartitionSpec as P

HD = 128
FF = 1536
QHEADS = 32
KVHEADS = 2
CTX = 4096
MB = 256
CAP = 16
EXPERT_AXES = ("y", "zh", "core")


def shifted(block, axis, distance):
    devices = range(lax.axis_size(axis))
    route = [((i - distance) % len(devices), i) for i in devices]
    return lax.ppermute(block, axis, route)


def swap(block, axis):
    return lax.ppermute(block, axis, [(0, 1), (1, 0)])


def body(stream, queries, keyvals, w_out, norm_gain, w_gate, w_up, w_down, routes, gate_scores):
    ny = lax.axis_size("y")
    nz = lax.axis_size("zh")
    nc = lax.axis_size("core")
    yi = lax.axis_index("y")
    zi = lax.axis_index("zh")
    ci = lax.axis_index("core")
    my_index = (yi * nz + zi) * nc + ci
    devices = ny * nz * nc
    tok_rows = stream.shape[1]
    residual = stream[0]
    residual_far = swap(residual, "zh")
    query_all = queries[0]
    proj_out = w_out[0]
    gain = norm_gain[0]
    gate_w = w_gate[0]
    up_w = w_up[0]
    down_w = w_down[0]
    heads_here = query_all.shape[1] // HD
    group = QHEADS // KVHEADS
    scale = 1.0 / math.sqrt(HD)
    block = keyvals.shape[1]

    kv = keyvals[0].reshape(block, KVHEADS, 2 * HD)
    rows_per_y = nz * nc * heads_here
    head_of_y = [y * rows_per_y // group for y in range(ny)]
    send_kv = jnp.stack([kv[:, h] for h in head_of_y])
    kv_y = lax.all_to_all(send_kv, "y", 0, 0, tiled=True)
    piece = jnp.stack([kv_y, swap(kv_y, "core")]).reshape(-1, 2 * HD)
    src_c = jnp.where(jnp.arange(2) == 0, ci, 1 - ci)[:, None]
    src_y = jnp.arange(ny)[None, :]
    src_block = (src_y * nz + zi) * nc + src_c
    key_pos = (src_block[..., None] * block + jnp.arange(block)[None, None, :]).reshape(-1)
    query_pos = CTX - MB + jnp.arange(MB, dtype=jnp.int32)
    visible = key_pos[None, :] <= query_pos[:, None]

    mine = query_all.reshape(MB, heads_here, HD).transpose(1, 0, 2)
    keys = piece[:, :HD]
    values = piece[:, HD:]

    def partial(query):
        score = jnp.einsum("hqd,kd->hqk", query, keys, preferred_element_type=jnp.float32) * scale
        top = jnp.max(jnp.where(visible[None], score, -1e30), axis=2, keepdims=True)
        weight = jnp.where(visible[None], jnp.exp(score - top), 0.0)
        total = jnp.sum(weight, axis=2, keepdims=True)
        summed = jnp.einsum(
            "hqk,kd->hqd", weight.astype(jnp.bfloat16), values, preferred_element_type=jnp.float32
        )
        return summed, top, total

    other_sum, other_top, other_total = partial(swap(mine, "zh"))
    far_sum, far_stats = swap(
        (other_sum.astype(jnp.bfloat16), jnp.concatenate([other_top, other_total], axis=2)), "zh"
    )
    near_sum, near_top, near_total = partial(mine)
    far_top = far_stats[:, :, 0:1]
    both_top = jnp.maximum(near_top, far_top)
    near_factor = jnp.exp(near_top - both_top)
    far_factor = jnp.exp(far_top - both_top)
    both_total = near_total * near_factor + far_stats[:, :, 1:2] * far_factor
    both_sum = near_sum * near_factor + far_sum.astype(jnp.float32) * far_factor
    heads = (both_sum / both_total).astype(jnp.bfloat16)
    heads = heads.transpose(1, 0, 2).reshape(MB, heads_here * HD)
    head_terms = jnp.dot(heads, proj_out, preferred_element_type=jnp.float32).astype(jnp.bfloat16)

    terms = head_terms.reshape(ny, nz, nc, tok_rows, -1)
    first = ci == 0
    keep_c = jnp.where(first, terms[:, :, 0], terms[:, :, 1])
    give_c = jnp.where(first, terms[:, :, 1], terms[:, :, 0])
    part_c = keep_c.astype(jnp.float32) + swap(give_c, "core").astype(jnp.float32)
    part_y = lax.all_to_all(part_c.astype(jnp.bfloat16), "y", 0, 0, tiled=True)
    part_y = jnp.sum(part_y.astype(jnp.float32), axis=0)
    keep_z = lax.dynamic_index_in_dim(part_y, zi, 0, keepdims=False)
    give_z = lax.dynamic_index_in_dim(part_y, 1 - zi, 0, keepdims=False)
    got = swap(jnp.stack([give_z, keep_z]).astype(jnp.bfloat16), "zh").astype(jnp.float32)
    attended = keep_z.astype(jnp.bfloat16).astype(jnp.float32) + got[0]
    attended_far = give_z.astype(jnp.bfloat16).astype(jnp.float32) + got[1]

    def norm(middle):
        return (
            middle * lax.rsqrt(jnp.mean(middle * middle, axis=1, keepdims=True) + 1e-06) * gain
        ).astype(jnp.bfloat16)

    middle = residual.astype(jnp.float32) + attended
    normed = norm(middle)
    normed_far = norm(residual_far.astype(jnp.float32) + attended_far)

    split = FF // gate_w.shape[1]
    experts_count = devices // split
    partner = (yi * nz + (1 - zi)) * nc + ci

    def plan(owner):
        chosen = lax.dynamic_slice_in_dim(routes[0], owner * tok_rows, tok_rows, 0)
        scores_in = lax.dynamic_slice_in_dim(gate_scores[0], owner * tok_rows, tok_rows, 0)
        onehot = chosen[:, :, None] == jnp.arange(experts_count, dtype=jnp.int32)[None, None, :]
        share = jnp.sum(jnp.where(onehot, scores_in[:, :, None], 0.0), axis=1) / jnp.sum(
            scores_in, axis=1, keepdims=True
        )
        routed = jnp.any(onehot, axis=1)
        slot = jnp.cumsum(routed.astype(jnp.int32), axis=0) - 1
        select = routed[None] & (slot[None] == jnp.arange(CAP)[:, None, None])
        select = select.transpose(2, 0, 1).reshape(experts_count * CAP, tok_rows)
        combine = select.T.astype(jnp.float32) * jnp.repeat(share, CAP, axis=1)
        return select.astype(jnp.bfloat16), combine

    select_own, combine_own = plan(my_index)
    select_far, combine_far = plan(partner)
    dispatch_own = jnp.dot(select_own, normed, preferred_element_type=jnp.float32)
    dispatch_far = jnp.dot(select_far, normed_far, preferred_element_type=jnp.float32)
    width = normed.shape[1]
    dispatch = jnp.stack(
        [dispatch_own.reshape(experts_count, CAP, width), dispatch_far.reshape(experts_count, CAP, width)],
        axis=1,
    ).astype(jnp.bfloat16)
    rows_y = lax.all_to_all(dispatch, "y", 0, 0, tiled=True)
    rows = jnp.stack([rows_y, swap(rows_y, "core")])
    flat = rows.reshape(-1, width)
    gate = jnp.dot(flat, gate_w, preferred_element_type=jnp.float32)
    upper = jnp.dot(flat, up_w, preferred_element_type=jnp.float32)
    activated = lax.optimization_barrier((jax.nn.silu(gate) * upper).astype(jnp.bfloat16))
    computed = (
        jnp.dot(activated, down_w, preferred_element_type=jnp.float32)
        .astype(jnp.bfloat16)
        .reshape(rows.shape)
    )

    chip_sum = computed[0].astype(jnp.float32) + swap(computed[1], "core").astype(jnp.float32)
    back = lax.all_to_all(chip_sum.astype(jnp.bfloat16), "y", 0, 0, tiled=True).astype(jnp.float32)
    hi = lax.Precision.HIGHEST
    combine_own = combine_own.reshape(tok_rows, experts_count, CAP)
    combine_far = combine_far.reshape(tok_rows, experts_count, CAP)
    mixed_own = jnp.einsum("txj,xjd->td", combine_own, back[:, 0], precision=hi)
    mixed_far = jnp.einsum("txj,xjd->td", combine_far, back[:, 1], precision=hi)
    own_part = shifted((middle + mixed_own).astype(jnp.bfloat16), "section", 1)
    sections = lax.axis_size("section")
    route = [
        (s * nz + z, ((s + 1) % sections) * nz + (nz - 1 - z)) for s in range(sections) for z in range(nz)
    ]
    far_part = lax.ppermute(mixed_far.astype(jnp.bfloat16), ("section", "zh"), route)
    layer_out = own_part.astype(jnp.float32) + far_part.astype(jnp.float32)
    return layer_out.astype(jnp.bfloat16)[None]


def solution(mesh):
    sizes = (mesh.shape["section"], 4, 2, 2)
    sub = Mesh(mesh.devices.reshape(sizes), ("section",) + EXPERT_AXES)
    ex = EXPERT_AXES
    return jax.shard_map(
        body,
        mesh=sub,
        in_specs=(
            P("section", ex, None),
            P("section", None, ex),
            P("section", ex, None),
            P("section", ex, None),
            P("section", None),
            P("section", None, ex),
            P("section", None, ex),
            P("section", ex, None),
            P("section", None, None),
            P("section", None, None),
        ),
        out_specs=P("section", ex, None),
        check_vma=False,
    )
```
